512 devices in a mesh: lon: 64 (over z_hi, y, core), lat: 8 (over z_lo, x).
Axes of the slice: x: 4, y: 8, z: 8 (z_hi: 4, z_lo: 2; z = z_hi * 2 + z_lo), core: 2. Of those that a mesh axis runs over, the one named last changes fastest.
Arguments:
- concentration: float32 [512, 1792, 128], P('lon', 'lat'), may hold values from -6 to 6
- wind: bfloat16 [3, 512, 1792, 128], P(None, 'lon', 'lat'), may hold values from -0.099609375 to 0.099609375
- kappa: bfloat16 [512, 1792, 128], P('lon', 'lat'), may hold values from 0.0099487305 to 0.059814453
- observed: bfloat16 [512, 1792, 128], P('lon', 'lat'), may hold values from -6 to 6
Outputs:
- grad_conc: float32 [512, 1792, 128], P('lon', 'lat')
- grad_kappa: float32 [512, 1792, 128], P('lon', 'lat')
The draws below stay inside these ranges and needn't reach their ends.
All inputs are finite; a program needn't handle non-finite values.
Results may differ from the reference program's by a relative error of at most 0.0023.
Values may be sent and summed in bfloat16 or wider, within the bound.
No kernel may reach another device: no remote copies, remote signals or barrier semaphores. Data moves between devices by JAX's collectives and lax.ppermute only.
A program may use at most 128 MiB of HBM per device.

```python
import math
import jax
import jax.numpy as jnp
from jax import lax

L = 128
NX = 512
NY = 1792


def shard_levels(rng, dims, split, smallest, high):
    level = 1.0
    for dim, shards_of in split:
        draws = jax.random.uniform(jax.random.fold_in(jax.random.fold_in(rng, 6), dim), (shards_of,), jnp.float32, smallest / len(split), high / len(split))
        level = level * jnp.repeat(jnp.exp(draws), dims[dim] // shards_of).reshape((-1,) + (1,) * (len(dims) - 1 - dim))
    return level


def normal_values(stream_key, extent, scale, limit, cuts=(), kind=jnp.bfloat16):
    values = scale * jax.random.normal(stream_key, extent, jnp.float32)
    if cuts:
        values = values * shard_levels(stream_key, extent, cuts, -0.22, 0.18)
    return jnp.clip(values, -limit, limit).astype(kind)


def setup_inputs(seed: int = 0) -> dict:
    splits = jax.random.split(jax.random.key(seed), 5)
    return {
        "concentration": normal_values(splits[0], (NX, NY, L), 1.0, 6.0, ((0, 64), (1, 8)), jnp.float32),
        "wind": jnp.clip(jax.random.uniform(splits[1], (3, NX, NY, L), jnp.float32, -0.099609375, 0.099609375) * shard_levels(splits[1], (3, NX, NY, L), ((1, 64), (2, 8)), -0.4, 0.0), -0.099609375, 0.099609375).astype(jnp.bfloat16),
        "kappa": jnp.clip(jnp.exp(math.log(0.059814453) - 1.7938024 * jax.random.uniform(splits[2], (NX, NY, L), jnp.float32) ** shard_levels(splits[2], (NX, NY, L), ((0, 64), (1, 8)), -0.2, 0.2)), 0.0099487305, 0.059814453).astype(jnp.bfloat16),
        "observed": normal_values(splits[3], (NX, NY, L), 1.0, 6.0, ((0, 64), (1, 8))),
    }


def coefs(speed, diffuse, opened):
    return ((jnp.maximum(speed, 0.0) + diffuse) * opened, (jnp.minimum(speed, 0.0) - diffuse) * opened)


def forward_nexts(field):
    zero_lat = jnp.zeros_like(field[:, :1])
    zero_lev = jnp.zeros_like(field[:, :, :1])
    return (jnp.roll(field, -1, 0), jnp.concatenate([field[:, 1:], zero_lat], 1), jnp.concatenate([field[:, :, 1:], zero_lev], 2))


def westward(faces):
    zero_lat = jnp.zeros_like(faces[1][:, :1])
    zero_lev = jnp.zeros_like(faces[2][:, :, :1])
    return (jnp.roll(faces[0], 1, 0), jnp.concatenate([zero_lat, faces[1][:, :-1]], 1), jnp.concatenate([zero_lev, faces[2][:, :, :-1]], 2))


def advance(conc, table):
    nexts = forward_nexts(conc)
    fluxes = tuple(pair[0] * conc + pair[1] * nearby for pair, nearby in zip(table, nexts))
    wests = westward(fluxes)
    return conc - (fluxes[0] + fluxes[1] + fluxes[2]) + (wests[0] + wests[1] + wests[2]), nexts


def retreat(adjoint, table):
    nexts = forward_nexts(adjoint)
    gaps = tuple(nearby - adjoint for nearby in nexts)
    parts = tuple(pair[1] * gap for pair, gap in zip(table, gaps))
    wests = westward(parts)
    gained = table[0][0] * gaps[0] + table[1][0] * gaps[1] + table[2][0] * gaps[2]
    return adjoint + gained + (wests[0] + wests[1] + wests[2]), gaps


def kappa_term(gaps, conc, nexts, north_open, upper_open):
    return gaps[0] * (conc - nexts[0]) + gaps[1] * (conc - nexts[1]) * north_open + gaps[2] * (conc - nexts[2]) * upper_open


def reference(concentration, wind, kappa, observed):
    speeds = wind.astype(jnp.float32)
    diffuse = kappa.astype(jnp.float32)
    north_open = (lax.broadcasted_iota(jnp.int32, (1, NY, 1), 1) < NY - 1).astype(jnp.float32)
    upper_open = (lax.broadcasted_iota(jnp.int32, (1, 1, L), 2) < L - 1).astype(jnp.float32)
    table = (coefs(speeds[0], diffuse, 1.0), coefs(speeds[1], diffuse, north_open), coefs(speeds[2], diffuse, upper_open))
    middle, nexts_first = advance(concentration, table)
    final, nexts_second = advance(middle, table)
    adjoint = final - observed.astype(jnp.float32)
    adjoint, gaps = retreat(adjoint, table)
    grad_kappa = kappa_term(gaps, middle, nexts_second, north_open, upper_open)
    grad_conc, gaps = retreat(adjoint, table)
    grad_kappa = grad_kappa + kappa_term(gaps, concentration, nexts_first, north_open, upper_open)
    return grad_conc, grad_kappa
```

```python
import jax
import jax.numpy as jnp
from jax import lax
from jax.sharding import PartitionSpec as P

HALO = 4


def passed_along(value, axis, steps, periodic):
    count = lax.axis_size(axis)
    if periodic:
        pairs = [(source, (source + steps) % count) for source in range(count)]
    else:
        pairs = [(source, source + steps) for source in range(count) if 0 <= source + steps < count]
    return lax.ppermute(value, axis, pairs)


def pad_rows(part, axis, before, after):
    widths = [(0, 0)] * part.ndim
    widths[axis] = (before, after)
    return jnp.pad(part, widths)


def lon_halo(fields, west_rows, east_rows):
    size = fields[0].shape[0]
    parts = {}
    for key, rows, start in (("east", east_rows, lambda e: 0), ("west", west_rows, lambda w: size - w)):
        pieces = [lax.slice_in_dim(f, start(r), start(r) + r, axis=0) for f, r in zip(fields, rows)]
        wide = pieces[0]
        narrow = jnp.concatenate(pieces[1:], 0)
        parts[key] = passed_along((wide, narrow), "lon", -1 if key == "east" else 1, True)
    out = []
    for key in ("east", "west"):
        wide, narrow = parts[key]
        rows = east_rows if key == "east" else west_rows
        got = [wide]
        at = 0
        for r in rows[1:]:
            got.append(narrow[at:at + r])
            at += r
        parts[key] = got
    for f, w, e, west, east in zip(fields, west_rows, east_rows, parts["west"], parts["east"]):
        west = pad_rows(west, 0, HALO - w, 0)
        east = pad_rows(east, 0, 0, HALO - e)
        out.append(jnp.concatenate([west, f, east], 0))
    return out


def lat_halo(fields):
    size = fields[0].shape[1]
    lows = jnp.stack([f[:, :HALO].astype(jnp.float32) for f in fields])
    highs = jnp.stack([f[:, size - HALO:].astype(jnp.float32) for f in fields])
    from_north = passed_along(lows, "lat", -1, False)
    from_south = passed_along(highs, "lat", 1, False)
    return [
        jnp.concatenate([from_south[n].astype(f.dtype), f, from_north[n].astype(f.dtype)], 1)
        for n, f in enumerate(fields)
    ]


def next_of(field, axis):
    if axis == 2:
        return jnp.concatenate([field[:, :, 1:], jnp.zeros_like(field[:, :, :1])], 2)
    size = field.shape[axis]
    return jnp.concatenate(
        [lax.slice_in_dim(field, 1, size, axis=axis), lax.slice_in_dim(field, size - 1, size, axis=axis)], axis
    )


def back_of(field, axis):
    if axis == 2:
        return jnp.concatenate([jnp.zeros_like(field[:, :, :1]), field[:, :, :-1]], 2)
    size = field.shape[axis]
    return jnp.concatenate(
        [lax.slice_in_dim(field, 0, 1, axis=axis), lax.slice_in_dim(field, 0, size - 1, axis=axis)], axis
    )


def advance(conc, table):
    nexts = tuple(next_of(conc, d) for d in range(3))
    fluxes = tuple(pair[0] * conc + pair[1] * nearby for pair, nearby in zip(table, nexts))
    wests = tuple(back_of(f, d) for d, f in enumerate(fluxes))
    return conc - (fluxes[0] + fluxes[1] + fluxes[2]) + (wests[0] + wests[1] + wests[2]), nexts


def retreat(adjoint, table):
    gaps = tuple(next_of(adjoint, d) - adjoint for d in range(3))
    parts = tuple(pair[1] * gap for pair, gap in zip(table, gaps))
    wests = tuple(back_of(p, d) for d, p in enumerate(parts))
    gained = table[0][0] * gaps[0] + table[1][0] * gaps[1] + table[2][0] * gaps[2]
    return adjoint + gained + (wests[0] + wests[1] + wests[2]), gaps


def kappa_term(gaps, conc, nexts, north_open, upper_open):
    return (
        gaps[0] * (conc - nexts[0])
        + gaps[1] * (conc - nexts[1]) * north_open
        + gaps[2] * (conc - nexts[2]) * upper_open
    )


def coefs(speed, diffuse, opened):
    return (
        (jnp.maximum(speed, 0.0) + diffuse) * opened,
        (jnp.minimum(speed, 0.0) - diffuse) * opened,
    )


def body(concentration, wind, kappa, observed):
    lon_rows, lat_rows, levels = concentration.shape
    lat_total = lat_rows * lax.axis_size("lat")
    fields = [concentration, wind[0], wind[1], wind[2], kappa, observed]
    west_rows = [4, 4, 4, 4, 4, 2]
    east_rows = [4, 3, 3, 3, 3, 2]
    fields = lon_halo(fields, west_rows, east_rows)
    fields = lat_halo(fields)
    conc, a0, a1, a2, kap, obs = fields
    ext_rows = conc.shape[1]

    upper_open = (lax.broadcasted_iota(jnp.int32, (1, 1, levels), 2) < levels - 1).astype(jnp.float32)
    lat_place = (
        lax.axis_index("lat") * lat_rows - HALO + lax.broadcasted_iota(jnp.int32, (1, ext_rows, 1), 1)
    )
    north_open = ((lat_place >= 0) & (lat_place < lat_total - 1)).astype(jnp.float32)
    diffuse = kap.astype(jnp.float32)
    table = (
        coefs(a0.astype(jnp.float32), diffuse, 1.0),
        coefs(a1.astype(jnp.float32), diffuse, north_open),
        coefs(a2.astype(jnp.float32), diffuse, upper_open),
    )
    middle, nexts_first = advance(conc, table)
    final, nexts_second = advance(middle, table)
    adjoint = final - obs.astype(jnp.float32)
    adjoint, gaps = retreat(adjoint, table)
    grad_kappa = kappa_term(gaps, middle, nexts_second, north_open, upper_open)
    grad_conc, gaps = retreat(adjoint, table)
    grad_kappa = grad_kappa + kappa_term(gaps, conc, nexts_first, north_open, upper_open)
    centre = (slice(HALO, HALO + lon_rows), slice(HALO, HALO + lat_rows), slice(None))
    return (grad_conc[centre], grad_kappa[centre])


def solution(mesh):
    return jax.shard_map(
        body,
        mesh=mesh,
        in_specs=(
            P("lon", "lat", None),
            P(None, "lon", "lat", None),
            P("lon", "lat", None),
            P("lon", "lat", None),
        ),
        out_specs=(P("lon", "lat", None), P("lon", "lat", None)),
        check_vma=False,
    )
```

```python
import jax
import jax.numpy as jnp
from jax import lax
from jax.experimental import pallas as pl
from jax.experimental.pallas import tpu as pltpu
from jax.sharding import PartitionSpec as P

HALO = 4
PAD = 8


def passed_along(value, axis, steps, periodic):
    count = lax.axis_size(axis)
    if periodic:
        pairs = [(source, (source + steps) % count) for source in range(count)]
    else:
        pairs = [(source, source + steps) for source in range(count) if 0 <= source + steps < count]
    return lax.ppermute(value, axis, pairs)


def pad_rows(part, axis, before, after):
    widths = [(0, 0)] * part.ndim
    widths[axis] = (before, after)
    return jnp.pad(part, widths)


def lon_halo(fields, west_rows, east_rows):
    size = fields[0].shape[0]
    parts = {}
    for key, rows, start in (("east", east_rows, lambda e: 0), ("west", west_rows, lambda w: size - w)):
        pieces = [lax.slice_in_dim(f, start(r), start(r) + r, axis=0) for f, r in zip(fields, rows)]
        wide = pieces[0]
        narrow = jnp.concatenate(pieces[1:], 0)
        parts[key] = passed_along((wide, narrow), "lon", -1 if key == "east" else 1, True)
    out = []
    for key in ("east", "west"):
        wide, narrow = parts[key]
        rows = east_rows if key == "east" else west_rows
        got = [wide]
        at = 0
        for r in rows[1:]:
            got.append(narrow[at:at + r])
            at += r
        parts[key] = got
    for f, w, e, west, east in zip(fields, west_rows, east_rows, parts["west"], parts["east"]):
        west = pad_rows(west, 0, HALO - w, 0)
        east = pad_rows(east, 0, 0, HALO - e)
        out.append(jnp.concatenate([west, f, east], 0))
    return out


def lat_halo(fields):
    size = fields[0].shape[1]
    lows = jnp.stack([f[:, :HALO].astype(jnp.float32) for f in fields])
    highs = jnp.stack([f[:, size - HALO:].astype(jnp.float32) for f in fields])
    from_north = passed_along(lows, "lat", -1, False)
    from_south = passed_along(highs, "lat", 1, False)
    out = []
    for n, f in enumerate(fields):
        gap = jnp.zeros(f.shape[:1] + (PAD - HALO,) + f.shape[2:], f.dtype)
        out.append(jnp.concatenate([gap, from_south[n].astype(f.dtype), f, from_north[n].astype(f.dtype), gap], 1))
    return out


def stencil_kernel(conc_ref, wind_ref, kappa_ref, obs_ref, north_ref, gc_ref, gk_ref,
                   own_ref, oth_ref, mid_ref, lam2_ref, lam1_ref):
    rows, lats, levels = conc_ref.shape
    f32 = jnp.float32
    north_open = north_ref[...]
    upper_open = (lax.broadcasted_iota(jnp.int32, (lats, levels), 1) < levels - 1).astype(f32)

    def next_lat(f):
        return pltpu.roll(f, lats - 1, 0)

    def back_lat(f):
        return pltpu.roll(f, 1, 0)

    def next_lev(f):
        return pltpu.roll(f, levels - 1, 1)

    def back_lev(f):
        return pltpu.roll(f, 1, 1)

    def coef_row(i, carry):
        diffuse = kappa_ref[i].astype(f32)
        for d, opened in ((0, None), (1, north_open), (2, upper_open)):
            speed = wind_ref[d, i].astype(f32)
            own = jnp.maximum(speed, 0.0) + diffuse
            oth = jnp.minimum(speed, 0.0) - diffuse
            if opened is not None:
                own = own * opened
                oth = oth * opened
            own_ref[d, i] = own
            oth_ref[d, i] = oth
        return carry

    lax.fori_loop(0, rows, coef_row, 0)

    def flux0(src, i):
        return own_ref[0, i] * src[i] + oth_ref[0, i] * src[i + 1]

    def advance(src, dst, lo, hi, minus=None):
        def row(i, west0):
            c = src[i]
            f0 = own_ref[0, i] * c + oth_ref[0, i] * src[i + 1]
            f1 = own_ref[1, i] * c + oth_ref[1, i] * next_lat(c)
            f2 = own_ref[2, i] * c + oth_ref[2, i] * next_lev(c)
            out = c - (f0 + f1 + f2) + (west0 + back_lat(f1) + back_lev(f2))
            if minus is not None:
                out = out - minus[i].astype(f32)
            dst[i] = out
            return f0

        lax.fori_loop(lo, hi, row, flux0(src, lo - 1))

    def part0(src, i):
        return oth_ref[0, i] * (src[i + 1] - src[i])

    def retreat_row(src, i, west0):
        lam = src[i]
        g0 = src[i + 1] - lam
        g1 = next_lat(lam) - lam
        g2 = next_lev(lam) - lam
        p0 = oth_ref[0, i] * g0
        p1 = oth_ref[1, i] * g1
        p2 = oth_ref[2, i] * g2
        gained = own_ref[0, i] * g0 + own_ref[1, i] * g1 + own_ref[2, i] * g2
        return lam + gained + (west0 + back_lat(p1) + back_lev(p2)), p0, (g0, g1, g2)

    def kappa_term(gaps, state, i):
        c = state[i]
        return (
            gaps[0] * (c - state[i + 1])
            + gaps[1] * (c - next_lat(c)) * north_open
            + gaps[2] * (c - next_lev(c)) * upper_open
        )

    h = (rows - gc_ref.shape[0]) // 2
    advance(conc_ref, mid_ref, 1, rows - 1)
    advance(mid_ref, lam2_ref, 2, rows - 2, minus=obs_ref)

    def lam1_row(i, west0):
        out, p0, _ = retreat_row(lam2_ref, i, west0)
        lam1_ref[i] = out
        return p0

    lax.fori_loop(3, rows - 3, lam1_row, part0(lam2_ref, 2))

    def last_row(i, west0):
        out, p0, gaps1 = retreat_row(lam1_ref, i, west0)
        lam = lam2_ref[i]
        gaps2 = (lam2_ref[i + 1] - lam, next_lat(lam) - lam, next_lev(lam) - lam)
        kappa = kappa_term(gaps2, mid_ref, i) + kappa_term(gaps1, conc_ref, i)
        gc_ref[i - h] = out[PAD:lats - PAD]
        gk_ref[i - h] = kappa[PAD:lats - PAD]
        return p0

    lax.fori_loop(h, rows - h, last_row, part0(lam1_ref, h - 1))


def body(concentration, wind, kappa, observed):
    lon_rows, lat_rows, levels = concentration.shape
    lat_total = lat_rows * lax.axis_size("lat")
    fields = [concentration, wind[0], wind[1], wind[2], kappa, observed]
    west_rows = [4, 4, 4, 4, 4, 2]
    east_rows = [4, 3, 3, 3, 3, 2]
    fields = lon_halo(fields, west_rows, east_rows)
    fields = lat_halo(fields)
    conc, a0, a1, a2, kap, obs = fields
    ext_rows, ext_lats = conc.shape[0], conc.shape[1]
    lat_place = lax.axis_index("lat") * lat_rows - PAD + lax.broadcasted_iota(jnp.int32, (ext_lats, levels), 0)
    north_open = ((lat_place >= 0) & (lat_place < lat_total - 1)).astype(jnp.float32)
    winds = jnp.stack([a0, a1, a2])
    whole = [conc, winds, kap, obs, north_open]
    vmem = pltpu.MemorySpace.VMEM
    state = pltpu.VMEM((ext_rows, ext_lats, levels), jnp.float32)
    return pl.pallas_call(
        stencil_kernel,
        out_shape=(
            jax.ShapeDtypeStruct((lon_rows, lat_rows, levels), jnp.float32),
            jax.ShapeDtypeStruct((lon_rows, lat_rows, levels), jnp.float32),
        ),
        in_specs=[pl.BlockSpec(memory_space=vmem) for _ in whole],
        out_specs=(pl.BlockSpec(memory_space=vmem), pl.BlockSpec(memory_space=vmem)),
        scratch_shapes=[
            pltpu.VMEM((3, ext_rows, ext_lats, levels), jnp.float32),
            pltpu.VMEM((3, ext_rows, ext_lats, levels), jnp.float32),
            state,
            state,
            state,
        ],
        compiler_params=pltpu.CompilerParams(vmem_limit_bytes=56 * 1024 * 1024),
    )(*whole)


def solution(mesh):
    return jax.shard_map(
        body,
        mesh=mesh,
        in_specs=(
            P("lon", "lat", None),
            P(None, "lon", "lat", None),
            P("lon", "lat", None),
            P("lon", "lat", None),
        ),
        out_specs=(P("lon", "lat", None), P("lon", "lat", None)),
        check_vma=False,
    )
```

```python
import functools

import jax
import jax.numpy as jnp
from jax import lax
from jax.experimental import pallas as pl
from jax.experimental.pallas import tpu as pltpu
from jax.sharding import PartitionSpec as P

HALO = 4
PAD = 8


def passed_along(value, axis, steps, periodic):
    count = lax.axis_size(axis)
    if periodic:
        pairs = [(source, (source + steps) % count) for source in range(count)]
    else:
        pairs = [(source, source + steps) for source in range(count) if 0 <= source + steps < count]
    return lax.ppermute(value, axis, pairs)


def pad_rows(part, axis, before, after):
    widths = [(0, 0)] * part.ndim
    widths[axis] = (before, after)
    return jnp.pad(part, widths)


def lon_halo(fields, west_rows, east_rows):
    size = fields[0].shape[0]
    got = {}
    for key, rows, steps in (("east", east_rows, -1), ("west", west_rows, 1)):
        start = (lambda r: 0) if key == "east" else (lambda r: size - r)
        pieces = [lax.slice_in_dim(f, start(r), start(r) + r, axis=0) for f, r in zip(fields, rows)]
        got[key] = passed_along((pieces[0], jnp.concatenate(pieces[1:], 0)), "lon", steps, True)
    return got


def unpack(wide, narrow, rows):
    out = [wide]
    at = 0
    for r in rows[1:]:
        out.append(narrow[at:at + r])
        at += r
    return out


def lat_halo(fields, west, east, west_rows, east_rows):
    def edge(part):
        rows = []
        for f, w, e, pw, pe in zip(fields, west_rows, east_rows, west, east):
            piece = jnp.concatenate([pad_rows(part(pw), 0, HALO - w, 0), part(f), pad_rows(part(pe), 0, 0, HALO - e)], 0)
            rows.append(piece.astype(jnp.float32))
        return jnp.stack(rows)

    size = fields[0].shape[1]
    lows = edge(lambda x: x[:, :HALO])
    highs = edge(lambda x: x[:, size - HALO:])
    return passed_along(highs, "lat", 1, False), passed_along(lows, "lat", -1, False)


def stencil_kernel(west_rows, east_rows, conc_in, wind_in, kappa_in, obs_in, west_c, west_p, east_c, east_p,
                   south_ref, north_halo, north_ref, gc_ref, gk_ref, raw_ref, own_ref, oth_ref, mid_ref, lam2_ref,
                   lam1_ref):
    fields, rows, lats, levels = raw_ref.shape
    block = conc_in.shape[0]
    f32 = jnp.float32
    north_open = north_ref[...]
    lo = PAD
    hi = lats - PAD
    gap = jnp.zeros((PAD - HALO, levels), f32)

    def put(f, r, core):
        raw_ref[f, r, lo:hi] = core
        raw_ref[f, r, lo - HALO:lo] = south_ref[f, r]
        raw_ref[f, r, hi:hi + HALO] = north_halo[f, r]
        raw_ref[f, r, :lo - HALO] = gap
        raw_ref[f, r, hi + HALO:] = gap

    def own_row(i, carry):
        put(0, i + HALO, conc_in[i])
        for d in range(3):
            put(1 + d, i + HALO, wind_in[d, i].astype(f32))
        put(4, i + HALO, kappa_in[i].astype(f32))
        put(5, i + HALO, obs_in[i].astype(f32))
        return carry

    lax.fori_loop(0, block, own_row, 0)
    empty = jnp.zeros((hi - lo, levels), f32)
    for r in range(HALO):
        put(0, r, west_c[r])
        put(0, HALO + block + r, east_c[r])
    at_w = 0
    at_e = 0
    for f in range(1, fields):
        w = west_rows[f]
        e = east_rows[f]
        for r in range(HALO):
            put(f, r, west_p[at_w + r - (HALO - w)].astype(f32) if r >= HALO - w else empty)
            put(f, HALO + block + r, east_p[at_e + r].astype(f32) if r < e else empty)
        at_w += w
        at_e += e
    conc_ref = raw_ref.at[0]
    obs_ref = raw_ref.at[5]
    upper_open = (lax.broadcasted_iota(jnp.int32, (lats, levels), 1) < levels - 1).astype(f32)

    def next_lat(f):
        return pltpu.roll(f, lats - 1, 0)

    def back_lat(f):
        return pltpu.roll(f, 1, 0)

    def next_lev(f):
        return pltpu.roll(f, levels - 1, 1)

    def back_lev(f):
        return pltpu.roll(f, 1, 1)

    def coef_row(i, carry):
        diffuse = raw_ref[4, i]
        for d, opened in ((0, None), (1, north_open), (2, upper_open)):
            speed = raw_ref[1 + d, i]
            own = jnp.maximum(speed, 0.0) + diffuse
            oth = jnp.minimum(speed, 0.0) - diffuse
            if opened is not None:
                own = own * opened
                oth = oth * opened
            own_ref[d, i] = own
            oth_ref[d, i] = oth
        return carry

    lax.fori_loop(0, rows, coef_row, 0)

    def flux0(src, i):
        return own_ref[0, i] * src[i] + oth_ref[0, i] * src[i + 1]

    def advance(src, dst, lo, hi, minus=None):
        def row(i, west0):
            c = src[i]
            f0 = own_ref[0, i] * c + oth_ref[0, i] * src[i + 1]
            f1 = own_ref[1, i] * c + oth_ref[1, i] * next_lat(c)
            f2 = own_ref[2, i] * c + oth_ref[2, i] * next_lev(c)
            out = c - (f0 + f1 + f2) + (west0 + back_lat(f1) + back_lev(f2))
            if minus is not None:
                out = out - minus[i]
            dst[i] = out
            return f0

        lax.fori_loop(lo, hi, row, flux0(src, lo - 1))

    def part0(src, i):
        return oth_ref[0, i] * (src[i + 1] - src[i])

    def retreat_row(src, i, west0):
        lam = src[i]
        g0 = src[i + 1] - lam
        g1 = next_lat(lam) - lam
        g2 = next_lev(lam) - lam
        p0 = oth_ref[0, i] * g0
        p1 = oth_ref[1, i] * g1
        p2 = oth_ref[2, i] * g2
        gained = own_ref[0, i] * g0 + own_ref[1, i] * g1 + own_ref[2, i] * g2
        return lam + gained + (west0 + back_lat(p1) + back_lev(p2)), p0, (g0, g1, g2)

    def kappa_term(gaps, state, i):
        c = state[i]
        return (
            gaps[0] * (c - state[i + 1])
            + gaps[1] * (c - next_lat(c)) * north_open
            + gaps[2] * (c - next_lev(c)) * upper_open
        )

    h = (rows - gc_ref.shape[0]) // 2
    advance(conc_ref, mid_ref, 1, rows - 1)
    advance(mid_ref, lam2_ref, 2, rows - 2, minus=obs_ref)

    def lam1_row(i, west0):
        out, p0, _ = retreat_row(lam2_ref, i, west0)
        lam1_ref[i] = out
        return p0

    lax.fori_loop(3, rows - 3, lam1_row, part0(lam2_ref, 2))

    def last_row(i, west0):
        out, p0, gaps1 = retreat_row(lam1_ref, i, west0)
        lam = lam2_ref[i]
        gaps2 = (lam2_ref[i + 1] - lam, next_lat(lam) - lam, next_lev(lam) - lam)
        kappa = kappa_term(gaps2, mid_ref, i) + kappa_term(gaps1, conc_ref, i)
        gc_ref[i - h] = out[PAD:lats - PAD]
        gk_ref[i - h] = kappa[PAD:lats - PAD]
        return p0

    lax.fori_loop(h, rows - h, last_row, part0(lam1_ref, h - 1))


def body(concentration, wind, kappa, observed):
    lon_rows, lat_rows, levels = concentration.shape
    lat_total = lat_rows * lax.axis_size("lat")
    fields = [concentration, wind[0], wind[1], wind[2], kappa, observed]
    west_rows = (4, 4, 3, 3, 4, 2)
    east_rows = (4, 3, 3, 3, 3, 2)
    got = lon_halo(fields, west_rows, east_rows)
    west = unpack(*got["west"], west_rows)
    east = unpack(*got["east"], east_rows)
    south, north = lat_halo(fields, west, east, west_rows, east_rows)
    ext_rows = lon_rows + 2 * HALO
    ext_lats = lat_rows + 2 * PAD
    lat_place = lax.axis_index("lat") * lat_rows - PAD + lax.broadcasted_iota(jnp.int32, (ext_lats, levels), 0)
    north_open = ((lat_place >= 0) & (lat_place < lat_total - 1)).astype(jnp.float32)
    whole = [concentration, wind, kappa, observed, *got["west"], *got["east"], south, north, north_open]
    vmem = pltpu.MemorySpace.VMEM
    state = pltpu.VMEM((ext_rows, ext_lats, levels), jnp.float32)
    return pl.pallas_call(
        functools.partial(stencil_kernel, west_rows, east_rows),
        out_shape=(
            jax.ShapeDtypeStruct((lon_rows, lat_rows, levels), jnp.float32),
            jax.ShapeDtypeStruct((lon_rows, lat_rows, levels), jnp.float32),
        ),
        in_specs=[pl.BlockSpec(memory_space=vmem) for _ in whole],
        out_specs=(pl.BlockSpec(memory_space=vmem), pl.BlockSpec(memory_space=vmem)),
        scratch_shapes=[
            pltpu.VMEM((len(fields), ext_rows, ext_lats, levels), jnp.float32),
            pltpu.VMEM((3, ext_rows, ext_lats, levels), jnp.float32),
            pltpu.VMEM((3, ext_rows, ext_lats, levels), jnp.float32),
            state,
            state,
            state,
        ],
        compiler_params=pltpu.CompilerParams(vmem_limit_bytes=60 * 1024 * 1024),
    )(*whole)


def solution(mesh):
    return jax.shard_map(
        body,
        mesh=mesh,
        in_specs=(
            P("lon", "lat", None),
            P(None, "lon", "lat", None),
            P("lon", "lat", None),
            P("lon", "lat", None),
        ),
        out_specs=(P("lon", "lat", None), P("lon", "lat", None)),
        check_vma=False,
    )
```

```python
import functools

import jax
import jax.numpy as jnp
from jax import lax
from jax.experimental import pallas as pl
from jax.experimental.pallas import tpu as pltpu
from jax.sharding import PartitionSpec as P

HALO = 4
PAD = 8


def passed_along(value, axis, steps, periodic):
    count = lax.axis_size(axis)
    if periodic:
        pairs = [(source, (source + steps) % count) for source in range(count)]
    else:
        pairs = [(source, source + steps) for source in range(count) if 0 <= source + steps < count]
    return lax.ppermute(value, axis, pairs)


def pad_rows(part, axis, before, after):
    widths = [(0, 0)] * part.ndim
    widths[axis] = (before, after)
    return jnp.pad(part, widths)


def lon_halo(fields, west_rows, east_rows):
    size = fields[0].shape[0]
    got = {}
    for key, rows, steps in (("east", east_rows, -1), ("west", west_rows, 1)):
        start = (lambda r: 0) if key == "east" else (lambda r: size - r)
        pieces = [lax.slice_in_dim(f, start(r), start(r) + r, axis=0) for f, r in zip(fields, rows)]
        high = pieces[0].astype(jnp.bfloat16)
        low = (pieces[0] - high.astype(jnp.float32)).astype(jnp.bfloat16)
        got[key] = passed_along(jnp.concatenate([high, low] + pieces[1:], 0), "lon", steps, True)
    return got


def unpack(pack, rows):
    out = [pack[:rows[0]].astype(jnp.float32) + pack[rows[0]:2 * rows[0]].astype(jnp.float32)]
    at = 2 * rows[0]
    for r in rows[1:]:
        out.append(pack[at:at + r])
        at += r
    return out


def lat_halo(fields, west, east, west_rows, east_rows):
    def edge(part):
        rows = []
        for f, w, e, pw, pe in zip(fields, west_rows, east_rows, west, east):
            piece = jnp.concatenate([pad_rows(part(pw), 0, HALO - w, 0), part(f), pad_rows(part(pe), 0, 0, HALO - e)], 0)
            rows.append(piece.astype(jnp.float32))
        return jnp.stack(rows)

    size = fields[0].shape[1]
    lows = edge(lambda x: x[:, :HALO])
    highs = edge(lambda x: x[:, size - HALO:])
    return passed_along(highs, "lat", 1, False), passed_along(lows, "lat", -1, False)


def stencil_kernel(west_rows, east_rows, conc_in, wind_in, kappa_in, obs_in, west_p, east_p,
                   south_ref, north_halo, north_ref, gc_ref, gk_ref, raw_ref, own_ref, oth_ref, mid_ref, lam2_ref,
                   lam1_ref):
    fields, rows, lats, levels = raw_ref.shape
    block = conc_in.shape[0]
    f32 = jnp.float32
    north_open = north_ref[...]
    lo = PAD
    hi = lats - PAD
    gap = jnp.zeros((PAD - HALO, levels), f32)

    def put(f, r, core):
        raw_ref[f, r, lo:hi] = core
        raw_ref[f, r, lo - HALO:lo] = south_ref[f, r]
        raw_ref[f, r, hi:hi + HALO] = north_halo[f, r]
        raw_ref[f, r, :lo - HALO] = gap
        raw_ref[f, r, hi + HALO:] = gap

    def own_row(i, carry):
        put(0, i + HALO, conc_in[i])
        for d in range(3):
            put(1 + d, i + HALO, wind_in[d, i].astype(f32))
        put(4, i + HALO, kappa_in[i].astype(f32))
        put(5, i + HALO, obs_in[i].astype(f32))
        return carry

    lax.fori_loop(0, block, own_row, 0)
    empty = jnp.zeros((hi - lo, levels), f32)
    for r in range(HALO):
        put(0, r, west_p[r].astype(f32) + west_p[HALO + r].astype(f32))
        put(0, HALO + block + r, east_p[r].astype(f32) + east_p[HALO + r].astype(f32))
    at_w = 2 * HALO
    at_e = 2 * HALO
    for f in range(1, fields):
        w = west_rows[f]
        e = east_rows[f]
        for r in range(HALO):
            put(f, r, west_p[at_w + r - (HALO - w)].astype(f32) if r >= HALO - w else empty)
            put(f, HALO + block + r, east_p[at_e + r].astype(f32) if r < e else empty)
        at_w += w
        at_e += e
    conc_ref = raw_ref.at[0]
    obs_ref = raw_ref.at[5]
    upper_open = (lax.broadcasted_iota(jnp.int32, (lats, levels), 1) < levels - 1).astype(f32)

    def next_lat(f):
        return pltpu.roll(f, lats - 1, 0)

    def back_lat(f):
        return pltpu.roll(f, 1, 0)

    def next_lev(f):
        return pltpu.roll(f, levels - 1, 1)

    def back_lev(f):
        return pltpu.roll(f, 1, 1)

    def coef_row(i, carry):
        diffuse = raw_ref[4, i]
        for d, opened in ((0, None), (1, north_open), (2, upper_open)):
            speed = raw_ref[1 + d, i]
            own = jnp.maximum(speed, 0.0) + diffuse
            oth = jnp.minimum(speed, 0.0) - diffuse
            if opened is not None:
                own = own * opened
                oth = oth * opened
            own_ref[d, i] = own
            oth_ref[d, i] = oth
        return carry

    lax.fori_loop(0, rows, coef_row, 0)

    def flux0(src, i):
        return own_ref[0, i] * src[i] + oth_ref[0, i] * src[i + 1]

    def advance(src, dst, lo, hi, minus=None):
        def row(i, west0):
            c = src[i]
            f0 = own_ref[0, i] * c + oth_ref[0, i] * src[i + 1]
            f1 = own_ref[1, i] * c + oth_ref[1, i] * next_lat(c)
            f2 = own_ref[2, i] * c + oth_ref[2, i] * next_lev(c)
            out = c - (f0 + f1 + f2) + (west0 + back_lat(f1) + back_lev(f2))
            if minus is not None:
                out = out - minus[i]
            dst[i] = out
            return f0

        lax.fori_loop(lo, hi, row, flux0(src, lo - 1))

    def part0(src, i):
        return oth_ref[0, i] * (src[i + 1] - src[i])

    def retreat_row(src, i, west0):
        lam = src[i]
        g0 = src[i + 1] - lam
        g1 = next_lat(lam) - lam
        g2 = next_lev(lam) - lam
        p0 = oth_ref[0, i] * g0
        p1 = oth_ref[1, i] * g1
        p2 = oth_ref[2, i] * g2
        gained = own_ref[0, i] * g0 + own_ref[1, i] * g1 + own_ref[2, i] * g2
        return lam + gained + (west0 + back_lat(p1) + back_lev(p2)), p0, (g0, g1, g2)

    def kappa_term(gaps, state, i):
        c = state[i]
        return (
            gaps[0] * (c - state[i + 1])
            + gaps[1] * (c - next_lat(c)) * north_open
            + gaps[2] * (c - next_lev(c)) * upper_open
        )

    h = (rows - gc_ref.shape[0]) // 2
    advance(conc_ref, mid_ref, 1, rows - 1)
    advance(mid_ref, lam2_ref, 2, rows - 2, minus=obs_ref)

    def lam1_row(i, west0):
        out, p0, _ = retreat_row(lam2_ref, i, west0)
        lam1_ref[i] = out
        return p0

    lax.fori_loop(3, rows - 3, lam1_row, part0(lam2_ref, 2))

    def last_row(i, west0):
        out, p0, gaps1 = retreat_row(lam1_ref, i, west0)
        lam = lam2_ref[i]
        gaps2 = (lam2_ref[i + 1] - lam, next_lat(lam) - lam, next_lev(lam) - lam)
        kappa = kappa_term(gaps2, mid_ref, i) + kappa_term(gaps1, conc_ref, i)
        gc_ref[i - h] = out[PAD:lats - PAD]
        gk_ref[i - h] = kappa[PAD:lats - PAD]
        return p0

    lax.fori_loop(h, rows - h, last_row, part0(lam1_ref, h - 1))


def body(concentration, wind, kappa, observed):
    lon_rows, lat_rows, levels = concentration.shape
    lat_total = lat_rows * lax.axis_size("lat")
    fields = [concentration, wind[0], wind[1], wind[2], kappa, observed]
    west_rows = (4, 4, 3, 3, 4, 2)
    east_rows = (4, 3, 3, 3, 3, 2)
    got = lon_halo(fields, west_rows, east_rows)
    west = unpack(got["west"], west_rows)
    east = unpack(got["east"], east_rows)
    south, north = lat_halo(fields, west, east, west_rows, east_rows)
    ext_rows = lon_rows + 2 * HALO
    ext_lats = lat_rows + 2 * PAD
    lat_place = lax.axis_index("lat") * lat_rows - PAD + lax.broadcasted_iota(jnp.int32, (ext_lats, levels), 0)
    north_open = ((lat_place >= 0) & (lat_place < lat_total - 1)).astype(jnp.float32)
    whole = [concentration, wind, kappa, observed, got["west"], got["east"], south, north, north_open]
    vmem = pltpu.MemorySpace.VMEM
    state = pltpu.VMEM((ext_rows, ext_lats, levels), jnp.float32)
    return pl.pallas_call(
        functools.partial(stencil_kernel, west_rows, east_rows),
        out_shape=(
            jax.ShapeDtypeStruct((lon_rows, lat_rows, levels), jnp.float32),
            jax.ShapeDtypeStruct((lon_rows, lat_rows, levels), jnp.float32),
        ),
        in_specs=[pl.BlockSpec(memory_space=vmem) for _ in whole],
        out_specs=(pl.BlockSpec(memory_space=vmem), pl.BlockSpec(memory_space=vmem)),
        scratch_shapes=[
            pltpu.VMEM((len(fields), ext_rows, ext_lats, levels), jnp.float32),
            pltpu.VMEM((3, ext_rows, ext_lats, levels), jnp.float32),
            pltpu.VMEM((3, ext_rows, ext_lats, levels), jnp.float32),
            state,
            state,
            state,
        ],
        compiler_params=pltpu.CompilerParams(vmem_limit_bytes=60 * 1024 * 1024),
    )(*whole)


def solution(mesh):
    return jax.shard_map(
        body,
        mesh=mesh,
        in_specs=(
            P("lon", "lat", None),
            P(None, "lon", "lat", None),
            P("lon", "lat", None),
            P("lon", "lat", None),
        ),
        out_specs=(P("lon", "lat", None), P("lon", "lat", None)),
        check_vma=False,
    )
```

```python
import functools

import jax
import jax.numpy as jnp
from jax import lax
from jax.experimental import pallas as pl
from jax.experimental.pallas import tpu as pltpu
from jax.sharding import PartitionSpec as P

HALO = 4
PAD = 8


def passed_along(value, axis, steps, periodic):
    count = lax.axis_size(axis)
    if periodic:
        pairs = [(source, (source + steps) % count) for source in range(count)]
    else:
        pairs = [(source, source + steps) for source in range(count) if 0 <= source + steps < count]
    return lax.ppermute(value, axis, pairs)


def pad_rows(part, axis, before, after):
    widths = [(0, 0)] * part.ndim
    widths[axis] = (before, after)
    return jnp.pad(part, widths)


def lon_halo(fields, west_rows, east_rows):
    size = fields[0].shape[0]
    got = {}
    for key, rows, steps in (("east", east_rows, -1), ("west", west_rows, 1)):
        start = (lambda r: 0) if key == "east" else (lambda r: size - r)
        pieces = [lax.slice_in_dim(f, start(r), start(r) + r, axis=0) for f, r in zip(fields, rows)]
        high = lax.reduce_precision(pieces[0], exponent_bits=8, mantissa_bits=7)
        low = pieces[0] - high
        parts = [high.astype(jnp.bfloat16), low.astype(jnp.bfloat16)] + pieces[1:]
        got[key] = passed_along(jnp.concatenate(parts, 0), "lon", steps, True)
    return got


def unpack(pack, rows):
    out = [pack[:rows[0]].astype(jnp.float32) + pack[rows[0]:2 * rows[0]].astype(jnp.float32)]
    at = 2 * rows[0]
    for r in rows[1:]:
        out.append(pack[at:at + r])
        at += r
    return out


def lat_halo(fields, west, east, west_rows, east_rows):
    def edge(part):
        rows = []
        for f, w, e, pw, pe in zip(fields, west_rows, east_rows, west, east):
            piece = jnp.concatenate([pad_rows(part(pw), 0, HALO - w, 0), part(f), pad_rows(part(pe), 0, 0, HALO - e)], 0)
            rows.append(piece.astype(jnp.float32))
        return jnp.stack(rows)

    size = fields[0].shape[1]
    lows = edge(lambda x: x[:, :HALO])
    highs = edge(lambda x: x[:, size - HALO:])
    return passed_along(highs, "lat", 1, False), passed_along(lows, "lat", -1, False)


def stencil_kernel(west_rows, east_rows, conc_in, wind_in, kappa_in, obs_in, west_p, east_p,
                   south_ref, north_halo, north_ref, gc_ref, gk_ref, raw_ref, own_ref, oth_ref, mid_ref, lam2_ref,
                   lam1_ref):
    fields, rows, lats, levels = raw_ref.shape
    block = conc_in.shape[0]
    f32 = jnp.float32
    north_open = north_ref[...]
    lo = PAD
    hi = lats - PAD
    gap = jnp.zeros((PAD - HALO, levels), f32)

    def put(f, r, core):
        raw_ref[f, r, lo:hi] = core
        raw_ref[f, r, lo - HALO:lo] = south_ref[f, r]
        raw_ref[f, r, hi:hi + HALO] = north_halo[f, r]
        raw_ref[f, r, :lo - HALO] = gap
        raw_ref[f, r, hi + HALO:] = gap

    def own_row(i, carry):
        put(0, i + HALO, conc_in[i])
        for d in range(3):
            put(1 + d, i + HALO, wind_in[d, i].astype(f32))
        put(4, i + HALO, kappa_in[i].astype(f32))
        put(5, i + HALO, obs_in[i].astype(f32))
        return carry

    lax.fori_loop(0, block, own_row, 0)
    empty = jnp.zeros((hi - lo, levels), f32)
    for r in range(HALO):
        put(0, r, west_p[r].astype(f32) + west_p[HALO + r].astype(f32))
        put(0, HALO + block + r, east_p[r].astype(f32) + east_p[HALO + r].astype(f32))
    at_w = 2 * HALO
    at_e = 2 * HALO
    for f in range(1, fields):
        w = west_rows[f]
        e = east_rows[f]
        for r in range(HALO):
            put(f, r, west_p[at_w + r - (HALO - w)].astype(f32) if r >= HALO - w else empty)
            put(f, HALO + block + r, east_p[at_e + r].astype(f32) if r < e else empty)
        at_w += w
        at_e += e
    conc_ref = raw_ref.at[0]
    obs_ref = raw_ref.at[5]
    upper_open = (lax.broadcasted_iota(jnp.int32, (lats, levels), 1) < levels - 1).astype(f32)

    def next_lat(f):
        return pltpu.roll(f, lats - 1, 0)

    def back_lat(f):
        return pltpu.roll(f, 1, 0)

    def next_lev(f):
        return pltpu.roll(f, levels - 1, 1)

    def back_lev(f):
        return pltpu.roll(f, 1, 1)

    def coef_row(i, carry):
        diffuse = raw_ref[4, i]
        for d, opened in ((0, None), (1, north_open), (2, upper_open)):
            speed = raw_ref[1 + d, i]
            own = jnp.maximum(speed, 0.0) + diffuse
            oth = jnp.minimum(speed, 0.0) - diffuse
            if opened is not None:
                own = own * opened
                oth = oth * opened
            own_ref[d, i] = own
            oth_ref[d, i] = oth
        return carry

    lax.fori_loop(0, rows, coef_row, 0)

    def flux0(src, i):
        return own_ref[0, i] * src[i] + oth_ref[0, i] * src[i + 1]

    def advance(src, dst, lo, hi, minus=None):
        def row(i, west0):
            c = src[i]
            f0 = own_ref[0, i] * c + oth_ref[0, i] * src[i + 1]
            f1 = own_ref[1, i] * c + oth_ref[1, i] * next_lat(c)
            f2 = own_ref[2, i] * c + oth_ref[2, i] * next_lev(c)
            out = c - (f0 + f1 + f2) + (west0 + back_lat(f1) + back_lev(f2))
            if minus is not None:
                out = out - minus[i]
            dst[i] = out
            return f0

        lax.fori_loop(lo, hi, row, flux0(src, lo - 1))

    def part0(src, i):
        return oth_ref[0, i] * (src[i + 1] - src[i])

    def retreat_row(src, i, west0):
        lam = src[i]
        g0 = src[i + 1] - lam
        g1 = next_lat(lam) - lam
        g2 = next_lev(lam) - lam
        p0 = oth_ref[0, i] * g0
        p1 = oth_ref[1, i] * g1
        p2 = oth_ref[2, i] * g2
        gained = own_ref[0, i] * g0 + own_ref[1, i] * g1 + own_ref[2, i] * g2
        return lam + gained + (west0 + back_lat(p1) + back_lev(p2)), p0, (g0, g1, g2)

    def kappa_term(gaps, state, i):
        c = state[i]
        return (
            gaps[0] * (c - state[i + 1])
            + gaps[1] * (c - next_lat(c)) * north_open
            + gaps[2] * (c - next_lev(c)) * upper_open
        )

    h = (rows - gc_ref.shape[0]) // 2
    advance(conc_ref, mid_ref, 1, rows - 1)
    advance(mid_ref, lam2_ref, 2, rows - 2, minus=obs_ref)

    def lam1_row(i, west0):
        out, p0, _ = retreat_row(lam2_ref, i, west0)
        lam1_ref[i] = out
        return p0

    lax.fori_loop(3, rows - 3, lam1_row, part0(lam2_ref, 2))

    def last_row(i, west0):
        out, p0, gaps1 = retreat_row(lam1_ref, i, west0)
        lam = lam2_ref[i]
        gaps2 = (lam2_ref[i + 1] - lam, next_lat(lam) - lam, next_lev(lam) - lam)
        kappa = kappa_term(gaps2, mid_ref, i) + kappa_term(gaps1, conc_ref, i)
        gc_ref[i - h] = out[PAD:lats - PAD]
        gk_ref[i - h] = kappa[PAD:lats - PAD]
        return p0

    lax.fori_loop(h, rows - h, last_row, part0(lam1_ref, h - 1))


def body(concentration, wind, kappa, observed):
    lon_rows, lat_rows, levels = concentration.shape
    lat_total = lat_rows * lax.axis_size("lat")
    fields = [concentration, wind[0], wind[1], wind[2], kappa, observed]
    west_rows = (4, 4, 3, 3, 4, 2)
    east_rows = (4, 3, 3, 3, 3, 2)
    got = lon_halo(fields, west_rows, east_rows)
    west = unpack(got["west"], west_rows)
    east = unpack(got["east"], east_rows)
    south, north = lat_halo(fields, west, east, west_rows, east_rows)
    ext_rows = lon_rows + 2 * HALO
    ext_lats = lat_rows + 2 * PAD
    lat_place = lax.axis_index("lat") * lat_rows - PAD + lax.broadcasted_iota(jnp.int32, (ext_lats, levels), 0)
    north_open = ((lat_place >= 0) & (lat_place < lat_total - 1)).astype(jnp.float32)
    whole = [concentration, wind, kappa, observed, got["west"], got["east"], south, north, north_open]
    vmem = pltpu.MemorySpace.VMEM
    state = pltpu.VMEM((ext_rows, ext_lats, levels), jnp.float32)
    return pl.pallas_call(
        functools.partial(stencil_kernel, west_rows, east_rows),
        out_shape=(
            jax.ShapeDtypeStruct((lon_rows, lat_rows, levels), jnp.float32),
            jax.ShapeDtypeStruct((lon_rows, lat_rows, levels), jnp.float32),
        ),
        in_specs=[pl.BlockSpec(memory_space=vmem) for _ in whole],
        out_specs=(pl.BlockSpec(memory_space=vmem), pl.BlockSpec(memory_space=vmem)),
        scratch_shapes=[
            pltpu.VMEM((len(fields), ext_rows, ext_lats, levels), jnp.float32),
            pltpu.VMEM((3, ext_rows, ext_lats, levels), jnp.float32),
            pltpu.VMEM((3, ext_rows, ext_lats, levels), jnp.float32),
            state,
            state,
            state,
        ],
        compiler_params=pltpu.CompilerParams(vmem_limit_bytes=60 * 1024 * 1024),
    )(*whole)


def solution(mesh):
    return jax.shard_map(
        body,
        mesh=mesh,
        in_specs=(
            P("lon", "lat", None),
            P(None, "lon", "lat", None),
            P("lon", "lat", None),
            P("lon", "lat", None),
        ),
        out_specs=(P("lon", "lat", None), P("lon", "lat", None)),
        check_vma=False,
    )
```

```python
import functools

import jax
import jax.numpy as jnp
from jax import lax
from jax.experimental import pallas as pl
from jax.experimental.pallas import tpu as pltpu
from jax.sharding import PartitionSpec as P

HALO = 4
PAD = 8


def passed_along(value, axis, steps, periodic):
    count = lax.axis_size(axis)
    if periodic:
        pairs = [(source, (source + steps) % count) for source in range(count)]
    else:
        pairs = [(source, source + steps) for source in range(count) if 0 <= source + steps < count]
    return lax.ppermute(value, axis, pairs)


def pad_rows(part, axis, before, after):
    widths = [(0, 0)] * part.ndim
    widths[axis] = (before, after)
    return jnp.pad(part, widths)


def lon_halo(fields, west_rows, east_rows):
    size = fields[0].shape[0]
    got = {}
    for key, rows, steps in (("east", east_rows, -1), ("west", west_rows, 1)):
        start = (lambda r: 0) if key == "east" else (lambda r: size - r)
        pieces = [lax.slice_in_dim(f, start(r), start(r) + r, axis=0) for f, r in zip(fields, rows)]
        high = lax.reduce_precision(pieces[0], exponent_bits=8, mantissa_bits=7)
        low = pieces[0] - high
        parts = [high.astype(jnp.bfloat16), low.astype(jnp.bfloat16)] + pieces[1:]
        got[key] = passed_along(jnp.concatenate(parts, 0), "lon", steps, True)
    return got


def unpack(pack, rows):
    out = [pack[:rows[0]].astype(jnp.float32) + pack[rows[0]:2 * rows[0]].astype(jnp.float32)]
    at = 2 * rows[0]
    for r in rows[1:]:
        out.append(pack[at:at + r])
        at += r
    return out


def lat_halo(fields, west, east, west_rows, east_rows):
    def edge(part):
        rows = []
        for f, w, e, pw, pe in zip(fields, west_rows, east_rows, west, east):
            piece = jnp.concatenate([pad_rows(part(pw), 0, HALO - w, 0), part(f), pad_rows(part(pe), 0, 0, HALO - e)], 0)
            rows.append(piece.astype(jnp.float32))
        return jnp.stack(rows)

    size = fields[0].shape[1]
    lows = edge(lambda x: x[:, :HALO])
    highs = edge(lambda x: x[:, size - HALO:])
    return passed_along(highs, "lat", 1, False), passed_along(lows, "lat", -1, False)


def stencil_kernel(west_rows, east_rows, layout, conc_in, wind_in, kappa_in, obs_in, west_p, east_p, south_ref,
                   north_halo, north_ref, *rest):
    own_at, south_at, north_at, out_at = layout
    gc_ref, gk_ref, raw_ref, own_ref, oth_ref, mid_ref, lam2_ref, lam1_ref = rest[-8:]
    fields, rows, lats, levels = raw_ref.shape
    block = conc_in.shape[0]
    own_n = conc_in.shape[1]
    out_n = gc_ref.shape[1]
    f32 = jnp.float32
    north_open = north_ref[...]
    covered = [(own_at, own_at + own_n)]
    if south_at is not None:
        covered.append((south_at, south_at + HALO))
    if north_at is not None:
        covered.append((north_at, north_at + HALO))
    covered.sort()
    gaps = []
    at = 0
    for lo, hi in covered:
        if lo > at:
            gaps.append((at, lo))
        at = hi
    if at < lats:
        gaps.append((at, lats))

    def put(f, r, core):
        raw_ref[f, r, own_at:own_at + own_n] = core
        if south_at is not None:
            raw_ref[f, r, south_at:south_at + HALO] = south_ref[f, r]
        if north_at is not None:
            raw_ref[f, r, north_at:north_at + HALO] = north_halo[f, r]
        for lo, hi in gaps:
            raw_ref[f, r, lo:hi] = jnp.zeros((hi - lo, levels), f32)

    def own_row(i, carry):
        put(0, i + HALO, conc_in[i])
        for d in range(3):
            put(1 + d, i + HALO, wind_in[d, i].astype(f32))
        put(4, i + HALO, kappa_in[i].astype(f32))
        put(5, i + HALO, obs_in[i].astype(f32))
        return carry

    lax.fori_loop(0, block, own_row, 0)
    empty = jnp.zeros((own_n, levels), f32)
    for r in range(HALO):
        put(0, r, west_p[r].astype(f32) + west_p[HALO + r].astype(f32))
        put(0, HALO + block + r, east_p[r].astype(f32) + east_p[HALO + r].astype(f32))
    at_w = 2 * HALO
    at_e = 2 * HALO
    for f in range(1, fields):
        w = west_rows[f]
        e = east_rows[f]
        for r in range(HALO):
            put(f, r, west_p[at_w + r - (HALO - w)].astype(f32) if r >= HALO - w else empty)
            put(f, HALO + block + r, east_p[at_e + r].astype(f32) if r < e else empty)
        at_w += w
        at_e += e
    conc_ref = raw_ref.at[0]
    obs_ref = raw_ref.at[5]
    upper_open = (lax.broadcasted_iota(jnp.int32, (lats, levels), 1) < levels - 1).astype(f32)

    def next_lat(f):
        return pltpu.roll(f, lats - 1, 0)

    def back_lat(f):
        return pltpu.roll(f, 1, 0)

    def next_lev(f):
        return pltpu.roll(f, levels - 1, 1)

    def back_lev(f):
        return pltpu.roll(f, 1, 1)

    def coef_row(i, carry):
        diffuse = raw_ref[4, i]
        for d, opened in ((0, None), (1, north_open), (2, upper_open)):
            speed = raw_ref[1 + d, i]
            own = jnp.maximum(speed, 0.0) + diffuse
            oth = jnp.minimum(speed, 0.0) - diffuse
            if opened is not None:
                own = own * opened
                oth = oth * opened
            own_ref[d, i] = own
            oth_ref[d, i] = oth
        return carry

    lax.fori_loop(0, rows, coef_row, 0)

    def flux0(src, i):
        return own_ref[0, i] * src[i] + oth_ref[0, i] * src[i + 1]

    def advance(src, dst, lo, hi, minus=None):
        def row(i, west0):
            c = src[i]
            f0 = own_ref[0, i] * c + oth_ref[0, i] * src[i + 1]
            f1 = own_ref[1, i] * c + oth_ref[1, i] * next_lat(c)
            f2 = own_ref[2, i] * c + oth_ref[2, i] * next_lev(c)
            out = c - (f0 + f1 + f2) + (west0 + back_lat(f1) + back_lev(f2))
            if minus is not None:
                out = out - minus[i]
            dst[i] = out
            return f0

        lax.fori_loop(lo, hi, row, flux0(src, lo - 1))

    def part0(src, i):
        return oth_ref[0, i] * (src[i + 1] - src[i])

    def retreat_row(src, i, west0):
        lam = src[i]
        g0 = src[i + 1] - lam
        g1 = next_lat(lam) - lam
        g2 = next_lev(lam) - lam
        p0 = oth_ref[0, i] * g0
        p1 = oth_ref[1, i] * g1
        p2 = oth_ref[2, i] * g2
        gained = own_ref[0, i] * g0 + own_ref[1, i] * g1 + own_ref[2, i] * g2
        return lam + gained + (west0 + back_lat(p1) + back_lev(p2)), p0, (g0, g1, g2)

    def kappa_term(gaps, state, i):
        c = state[i]
        return (
            gaps[0] * (c - state[i + 1])
            + gaps[1] * (c - next_lat(c)) * north_open
            + gaps[2] * (c - next_lev(c)) * upper_open
        )

    h = (rows - gc_ref.shape[0]) // 2
    advance(conc_ref, mid_ref, 1, rows - 1)
    advance(mid_ref, lam2_ref, 2, rows - 2, minus=obs_ref)

    def lam1_row(i, west0):
        out, p0, _ = retreat_row(lam2_ref, i, west0)
        lam1_ref[i] = out
        return p0

    lax.fori_loop(3, rows - 3, lam1_row, part0(lam2_ref, 2))

    def last_row(i, west0):
        out, p0, gaps1 = retreat_row(lam1_ref, i, west0)
        lam = lam2_ref[i]
        gaps2 = (lam2_ref[i + 1] - lam, next_lat(lam) - lam, next_lev(lam) - lam)
        kappa = kappa_term(gaps2, mid_ref, i) + kappa_term(gaps1, conc_ref, i)
        gc_ref[i - h] = out[out_at:out_at + out_n]
        gk_ref[i - h] = kappa[out_at:out_at + out_n]
        return p0

    lax.fori_loop(h, rows - h, last_row, part0(lam1_ref, h - 1))


def body(concentration, wind, kappa, observed):
    lon_rows, lat_rows, levels = concentration.shape
    lat_total = lat_rows * lax.axis_size("lat")
    fields = [concentration, wind[0], wind[1], wind[2], kappa, observed]
    west_rows = (4, 4, 3, 3, 4, 2)
    east_rows = (4, 3, 3, 3, 3, 2)
    got = lon_halo(fields, west_rows, east_rows)
    west = unpack(got["west"], west_rows)
    east = unpack(got["east"], east_rows)
    south, north = lat_halo(fields, west, east, west_rows, east_rows)
    ext_rows = lon_rows + 2 * HALO
    ext_lats = lat_rows + 2 * PAD
    lat_place = lax.axis_index("lat") * lat_rows - PAD + lax.broadcasted_iota(jnp.int32, (ext_lats, levels), 0)
    north_open = ((lat_place >= 0) & (lat_place < lat_total - 1)).astype(jnp.float32)
    packs = [got["west"], got["east"]]
    own = [concentration, wind, kappa, observed]
    vmem = pltpu.MemorySpace.VMEM
    out_type = jax.ShapeDtypeStruct((lon_rows, lat_rows, levels), jnp.float32)

    def scratch(window):
        state = pltpu.VMEM((ext_rows, window, levels), jnp.float32)
        return [
            pltpu.VMEM((len(fields), ext_rows, window, levels), jnp.float32),
            pltpu.VMEM((3, ext_rows, window, levels), jnp.float32),
            pltpu.VMEM((3, ext_rows, window, levels), jnp.float32),
            state,
            state,
            state,
        ]

    empty_halo = jnp.zeros_like(north)
    whole = own + packs + [empty_halo, empty_halo, north_open]
    grad_conc, grad_kappa = pl.pallas_call(
        functools.partial(stencil_kernel, west_rows, east_rows, (PAD, None, None, PAD)),
        out_shape=(out_type, out_type),
        in_specs=[pl.BlockSpec(memory_space=vmem) for _ in whole],
        out_specs=(pl.BlockSpec(memory_space=vmem), pl.BlockSpec(memory_space=vmem)),
        scratch_shapes=scratch(ext_lats),
        compiler_params=pltpu.CompilerParams(vmem_limit_bytes=60 * 1024 * 1024),
    )(*whole)

    strip = 2 * PAD
    window = 3 * PAD
    for side in ("south", "north"):
        if side == "south":
            layout = (PAD, PAD - HALO, None, PAD)
            first = 0
            mask = north_open[:window]
        else:
            layout = (0, None, strip, PAD)
            first = lat_rows - strip
            mask = north_open[ext_lats - window:]
        out_block = first // PAD + (0 if side == "south" else 1)
        in_block = first // strip

        def rows_of(array, lead):
            shape = array.shape[:lead] + (strip, levels)
            return pl.BlockSpec(shape, lambda i, lead=lead: (0,) * lead + (in_block, 0))

        args = own + packs + [south, north, mask, grad_conc, grad_kappa]
        specs = [rows_of(a, a.ndim - 2) for a in own + packs]
        specs += [pl.BlockSpec(memory_space=vmem)] * 3 + [pl.BlockSpec(memory_space=pl.ANY)] * 2
        out_spec = pl.BlockSpec((lon_rows, PAD, levels), lambda i: (0, out_block, 0))
        grad_conc, grad_kappa = pl.pallas_call(
            functools.partial(stencil_kernel, west_rows, east_rows, layout),
            out_shape=(out_type, out_type),
            grid=(1,),
            in_specs=specs,
            out_specs=(out_spec, out_spec),
            scratch_shapes=scratch(window),
            input_output_aliases={len(args) - 2: 0, len(args) - 1: 1},
        )(*args)
    return grad_conc, grad_kappa


def solution(mesh):
    return jax.shard_map(
        body,
        mesh=mesh,
        in_specs=(
            P("lon", "lat", None),
            P(None, "lon", "lat", None),
            P("lon", "lat", None),
            P("lon", "lat", None),
        ),
        out_specs=(P("lon", "lat", None), P("lon", "lat", None)),
        check_vma=False,
    )
```

```python
import functools

import jax
import jax.numpy as jnp
from jax import lax
from jax.experimental import pallas as pl
from jax.experimental.pallas import tpu as pltpu
from jax.sharding import PartitionSpec as P

HALO = 4
PAD = 8


def passed_along(value, axis, steps, periodic):
    count = lax.axis_size(axis)
    if periodic:
        pairs = [(source, (source + steps) % count) for source in range(count)]
    else:
        pairs = [(source, source + steps) for source in range(count) if 0 <= source + steps < count]
    return lax.ppermute(value, axis, pairs)


def pad_rows(part, axis, before, after):
    widths = [(0, 0)] * part.ndim
    widths[axis] = (before, after)
    return jnp.pad(part, widths)


def lon_halo(fields, west_rows, east_rows):
    size = fields[0].shape[0]
    got = {}
    for key, rows, steps in (("east", east_rows, -1), ("west", west_rows, 1)):
        start = (lambda r: 0) if key == "east" else (lambda r: size - r)
        pieces = [lax.slice_in_dim(f, start(r), start(r) + r, axis=0) for f, r in zip(fields, rows)]
        high = lax.reduce_precision(pieces[0], exponent_bits=8, mantissa_bits=7)
        low = pieces[0] - high
        parts = [high.astype(jnp.bfloat16), low.astype(jnp.bfloat16)] + pieces[1:]
        got[key] = passed_along(jnp.concatenate(parts, 0), "lon", steps, True)
    return got


def unpack(pack, rows):
    out = [pack[:rows[0]].astype(jnp.float32) + pack[rows[0]:2 * rows[0]].astype(jnp.float32)]
    at = 2 * rows[0]
    for r in rows[1:]:
        out.append(pack[at:at + r])
        at += r
    return out


def lat_halo(fields, west_rows, east_rows):
    size = fields[0].shape[1]
    lows = jnp.stack([f[:, :HALO].astype(jnp.float32) for f in fields])
    highs = jnp.stack([f[:, size - HALO:].astype(jnp.float32) for f in fields])
    from_south = passed_along(highs, "lat", 1, False)
    from_north = passed_along(lows, "lat", -1, False)
    both = jnp.stack([from_south, from_north])
    block = fields[0].shape[0]
    west = passed_along(both[:, :, block - HALO:], "lon", 1, True)
    east = passed_along(both[:, :, :HALO], "lon", -1, True)
    return [jnp.concatenate([west[n], both[n], east[n]], 1) for n in range(2)]


def stencil_kernel(west_rows, east_rows, conc_in, wind_in, kappa_in, obs_in, west_p, east_p,
                   south_ref, north_halo, north_ref, gc_ref, gk_ref, raw_ref, own_ref, oth_ref, mid_ref, lam2_ref,
                   lam1_ref):
    fields, rows, lats, levels = raw_ref.shape
    block = conc_in.shape[0]
    f32 = jnp.float32
    north_open = north_ref[...]
    lo = PAD
    hi = lats - PAD
    gap = jnp.zeros((PAD - HALO, levels), f32)

    def put(f, r, core):
        raw_ref[f, r, lo:hi] = core
        raw_ref[f, r, lo - HALO:lo] = south_ref[f, r]
        raw_ref[f, r, hi:hi + HALO] = north_halo[f, r]
        raw_ref[f, r, :lo - HALO] = gap
        raw_ref[f, r, hi + HALO:] = gap

    def own_row(i, carry):
        put(0, i + HALO, conc_in[i])
        for d in range(3):
            put(1 + d, i + HALO, wind_in[d, i].astype(f32))
        put(4, i + HALO, kappa_in[i].astype(f32))
        put(5, i + HALO, obs_in[i].astype(f32))
        return carry

    lax.fori_loop(0, block, own_row, 0)
    empty = jnp.zeros((hi - lo, levels), f32)
    for r in range(HALO):
        put(0, r, west_p[r].astype(f32) + west_p[HALO + r].astype(f32))
        put(0, HALO + block + r, east_p[r].astype(f32) + east_p[HALO + r].astype(f32))
    at_w = 2 * HALO
    at_e = 2 * HALO
    for f in range(1, fields):
        w = west_rows[f]
        e = east_rows[f]
        for r in range(HALO):
            put(f, r, west_p[at_w + r - (HALO - w)].astype(f32) if r >= HALO - w else empty)
            put(f, HALO + block + r, east_p[at_e + r].astype(f32) if r < e else empty)
        at_w += w
        at_e += e
    conc_ref = raw_ref.at[0]
    obs_ref = raw_ref.at[5]
    upper_open = (lax.broadcasted_iota(jnp.int32, (lats, levels), 1) < levels - 1).astype(f32)

    def next_lat(f):
        return pltpu.roll(f, lats - 1, 0)

    def back_lat(f):
        return pltpu.roll(f, 1, 0)

    def next_lev(f):
        return pltpu.roll(f, levels - 1, 1)

    def back_lev(f):
        return pltpu.roll(f, 1, 1)

    def coef_row(i, carry):
        diffuse = raw_ref[4, i]
        for d, opened in ((0, None), (1, north_open), (2, upper_open)):
            speed = raw_ref[1 + d, i]
            own = jnp.maximum(speed, 0.0) + diffuse
            oth = jnp.minimum(speed, 0.0) - diffuse
            if opened is not None:
                own = own * opened
                oth = oth * opened
            own_ref[d, i] = own
            oth_ref[d, i] = oth
        return carry

    lax.fori_loop(0, rows, coef_row, 0)

    def flux0(src, i):
        return own_ref[0, i] * src[i] + oth_ref[0, i] * src[i + 1]

    def advance(src, dst, lo, hi, minus=None):
        def row(i, west0):
            c = src[i]
            f0 = own_ref[0, i] * c + oth_ref[0, i] * src[i + 1]
            f1 = own_ref[1, i] * c + oth_ref[1, i] * next_lat(c)
            f2 = own_ref[2, i] * c + oth_ref[2, i] * next_lev(c)
            out = c - (f0 + f1 + f2) + (west0 + back_lat(f1) + back_lev(f2))
            if minus is not None:
                out = out - minus[i]
            dst[i] = out
            return f0

        lax.fori_loop(lo, hi, row, flux0(src, lo - 1))

    def part0(src, i):
        return oth_ref[0, i] * (src[i + 1] - src[i])

    def retreat_row(src, i, west0):
        lam = src[i]
        g0 = src[i + 1] - lam
        g1 = next_lat(lam) - lam
        g2 = next_lev(lam) - lam
        p0 = oth_ref[0, i] * g0
        p1 = oth_ref[1, i] * g1
        p2 = oth_ref[2, i] * g2
        gained = own_ref[0, i] * g0 + own_ref[1, i] * g1 + own_ref[2, i] * g2
        return lam + gained + (west0 + back_lat(p1) + back_lev(p2)), p0, (g0, g1, g2)

    def kappa_term(gaps, state, i):
        c = state[i]
        return (
            gaps[0] * (c - state[i + 1])
            + gaps[1] * (c - next_lat(c)) * north_open
            + gaps[2] * (c - next_lev(c)) * upper_open
        )

    h = (rows - gc_ref.shape[0]) // 2
    advance(conc_ref, mid_ref, 1, rows - 1)
    advance(mid_ref, lam2_ref, 2, rows - 2, minus=obs_ref)

    def lam1_row(i, west0):
        out, p0, _ = retreat_row(lam2_ref, i, west0)
        lam1_ref[i] = out
        return p0

    lax.fori_loop(3, rows - 3, lam1_row, part0(lam2_ref, 2))

    def last_row(i, west0):
        out, p0, gaps1 = retreat_row(lam1_ref, i, west0)
        lam = lam2_ref[i]
        gaps2 = (lam2_ref[i + 1] - lam, next_lat(lam) - lam, next_lev(lam) - lam)
        kappa = kappa_term(gaps2, mid_ref, i) + kappa_term(gaps1, conc_ref, i)
        gc_ref[i - h] = out[PAD:lats - PAD]
        gk_ref[i - h] = kappa[PAD:lats - PAD]
        return p0

    lax.fori_loop(h, rows - h, last_row, part0(lam1_ref, h - 1))


def body(concentration, wind, kappa, observed):
    lon_rows, lat_rows, levels = concentration.shape
    lat_total = lat_rows * lax.axis_size("lat")
    fields = [concentration, wind[0], wind[1], wind[2], kappa, observed]
    west_rows = (4, 4, 3, 3, 4, 2)
    east_rows = (4, 3, 3, 3, 3, 2)
    got = lon_halo(fields, west_rows, east_rows)
    south, north = lat_halo(fields, west_rows, east_rows)
    ext_rows = lon_rows + 2 * HALO
    ext_lats = lat_rows + 2 * PAD
    lat_place = lax.axis_index("lat") * lat_rows - PAD + lax.broadcasted_iota(jnp.int32, (ext_lats, levels), 0)
    north_open = ((lat_place >= 0) & (lat_place < lat_total - 1)).astype(jnp.float32)
    whole = [concentration, wind, kappa, observed, got["west"], got["east"], south, north, north_open]
    vmem = pltpu.MemorySpace.VMEM
    state = pltpu.VMEM((ext_rows, ext_lats, levels), jnp.float32)
    return pl.pallas_call(
        functools.partial(stencil_kernel, west_rows, east_rows),
        out_shape=(
            jax.ShapeDtypeStruct((lon_rows, lat_rows, levels), jnp.float32),
            jax.ShapeDtypeStruct((lon_rows, lat_rows, levels), jnp.float32),
        ),
        in_specs=[pl.BlockSpec(memory_space=vmem) for _ in whole],
        out_specs=(pl.BlockSpec(memory_space=vmem), pl.BlockSpec(memory_space=vmem)),
        scratch_shapes=[
            pltpu.VMEM((len(fields), ext_rows, ext_lats, levels), jnp.float32),
            pltpu.VMEM((3, ext_rows, ext_lats, levels), jnp.float32),
            pltpu.VMEM((3, ext_rows, ext_lats, levels), jnp.float32),
            state,
            state,
            state,
        ],
        compiler_params=pltpu.CompilerParams(vmem_limit_bytes=60 * 1024 * 1024),
    )(*whole)


def solution(mesh):
    return jax.shard_map(
        body,
        mesh=mesh,
        in_specs=(
            P("lon", "lat", None),
            P(None, "lon", "lat", None),
            P("lon", "lat", None),
            P("lon", "lat", None),
        ),
        out_specs=(P("lon", "lat", None), P("lon", "lat", None)),
        check_vma=False,
    )
```

```python
import functools

import jax
import jax.numpy as jnp
from jax import lax
from jax.experimental import pallas as pl
from jax.experimental.pallas import tpu as pltpu
from jax.sharding import PartitionSpec as P


HALO = 4
PAD = 8


def passed_along(value, axis, steps, periodic):
    count = lax.axis_size(axis)
    if periodic:
        pairs = [(source, (source + steps) % count) for source in range(count)]
    else:
        pairs = [(source, source + steps) for source in range(count) if 0 <= source + steps < count]
    return lax.ppermute(value, axis, pairs)


def lon_halo(fields, west_rows, east_rows):
    size = fields[0].shape[0]
    got = {}
    for key, rows, steps in (("east", east_rows, -1), ("west", west_rows, 1)):
        start = (lambda r: 0) if key == "east" else (lambda r: size - r)
        pieces = [lax.slice_in_dim(f, start(r), start(r) + r, axis=0) for f, r in zip(fields, rows)]
        high = lax.reduce_precision(pieces[0], exponent_bits=8, mantissa_bits=7)
        low = pieces[0] - high
        parts = [high.astype(jnp.bfloat16), low.astype(jnp.bfloat16)] + pieces[1:]
        got[key] = passed_along(jnp.concatenate(parts, 0), "lon", steps, True)
    return got


def lat_halo(fields):
    size = fields[0].shape[1]
    lows = jnp.stack([f[:, :HALO].astype(jnp.float32) for f in fields])
    highs = jnp.stack([f[:, size - HALO:].astype(jnp.float32) for f in fields])
    from_south = passed_along(highs, "lat", 1, False)
    from_north = passed_along(lows, "lat", -1, False)
    both = jnp.stack([from_south, from_north])
    block = fields[0].shape[0]
    west = passed_along(both[:, :, block - HALO:], "lon", 1, True)
    east = passed_along(both[:, :, :HALO], "lon", -1, True)
    return [jnp.concatenate([west[n], both[n], east[n]], 1) for n in range(2)]


def stencil_kernel(west_rows, east_rows, conc_in, wind_in, kappa_in, obs_in, west_p, east_p,
                   south_ref, north_halo, north_ref, gc_ref, gk_ref, raw_ref, own_ref, oth_ref, mid_ref, lam2_ref,
                   lam1_ref):
    fields, rows, lats, levels = raw_ref.shape
    block = conc_in.shape[0]
    f32 = jnp.float32
    north_open = north_ref[...]
    lo = PAD
    hi = lats - PAD
    gap = jnp.zeros((PAD - HALO, levels), f32)

    def put(f, r, core):
        raw_ref[f, r, lo:hi] = core
        raw_ref[f, r, lo - HALO:lo] = south_ref[f, r]
        raw_ref[f, r, hi:hi + HALO] = north_halo[f, r]
        raw_ref[f, r, :lo - HALO] = gap
        raw_ref[f, r, hi + HALO:] = gap

    def own_row(i, carry):
        put(0, i + HALO, conc_in[i])
        for d in range(3):
            put(1 + d, i + HALO, wind_in[d, i].astype(f32))
        put(4, i + HALO, kappa_in[i].astype(f32))
        put(5, i + HALO, obs_in[i].astype(f32))
        return carry

    lax.fori_loop(0, block, own_row, 0)
    empty = jnp.zeros((hi - lo, levels), f32)
    for r in range(HALO):
        put(0, r, west_p[r].astype(f32) + west_p[HALO + r].astype(f32))
        put(0, HALO + block + r, east_p[r].astype(f32) + east_p[HALO + r].astype(f32))
    at_w = 2 * HALO
    at_e = 2 * HALO
    for f in range(1, fields):
        w = west_rows[f]
        e = east_rows[f]
        for r in range(HALO):
            put(f, r, west_p[at_w + r - (HALO - w)].astype(f32) if r >= HALO - w else empty)
            put(f, HALO + block + r, east_p[at_e + r].astype(f32) if r < e else empty)
        at_w += w
        at_e += e
    conc_ref = raw_ref.at[0]
    obs_ref = raw_ref.at[5]
    upper_open = (lax.broadcasted_iota(jnp.int32, (lats, levels), 1) < levels - 1).astype(f32)

    def next_lat(f):
        return pltpu.roll(f, lats - 1, 0)

    def back_lat(f):
        return pltpu.roll(f, 1, 0)

    def next_lev(f):
        return pltpu.roll(f, levels - 1, 1)

    def back_lev(f):
        return pltpu.roll(f, 1, 1)

    def coef_row(i, carry):
        diffuse = raw_ref[4, i]
        for d, opened in ((0, None), (1, north_open), (2, upper_open)):
            speed = raw_ref[1 + d, i]
            own = jnp.maximum(speed, 0.0) + diffuse
            oth = jnp.minimum(speed, 0.0) - diffuse
            if opened is not None:
                own = own * opened
                oth = oth * opened
            own_ref[d, i] = own
            oth_ref[d, i] = oth
        return carry

    lax.fori_loop(0, rows, coef_row, 0)

    def flux0(src, i):
        return own_ref[0, i] * src[i] + oth_ref[0, i] * src[i + 1]

    def advance(src, dst, lo, hi, minus=None):
        def row(i, west0):
            c = src[i]
            f0 = own_ref[0, i] * c + oth_ref[0, i] * src[i + 1]
            f1 = own_ref[1, i] * c + oth_ref[1, i] * next_lat(c)
            f2 = own_ref[2, i] * c + oth_ref[2, i] * next_lev(c)
            out = c - (f0 + f1 + f2) + (west0 + back_lat(f1) + back_lev(f2))
            if minus is not None:
                out = out - minus[i]
            dst[i] = out
            return f0

        lax.fori_loop(lo, hi, row, flux0(src, lo - 1))

    def part0(src, i):
        return oth_ref[0, i] * (src[i + 1] - src[i])

    def retreat_row(src, i, west0):
        lam = src[i]
        g0 = src[i + 1] - lam
        g1 = next_lat(lam) - lam
        g2 = next_lev(lam) - lam
        p0 = oth_ref[0, i] * g0
        p1 = oth_ref[1, i] * g1
        p2 = oth_ref[2, i] * g2
        gained = own_ref[0, i] * g0 + own_ref[1, i] * g1 + own_ref[2, i] * g2
        return lam + gained + (west0 + back_lat(p1) + back_lev(p2)), p0, (g0, g1, g2)

    def kappa_term(gaps, state, i):
        c = state[i]
        return (
            gaps[0] * (c - state[i + 1])
            + gaps[1] * (c - next_lat(c)) * north_open
            + gaps[2] * (c - next_lev(c)) * upper_open
        )

    h = (rows - gc_ref.shape[0]) // 2
    advance(conc_ref, mid_ref, 1, rows - 1)
    advance(mid_ref, lam2_ref, 2, rows - 2, minus=obs_ref)

    def lam1_row(i, west0):
        out, p0, _ = retreat_row(lam2_ref, i, west0)
        lam1_ref[i] = out
        return p0

    lax.fori_loop(3, rows - 3, lam1_row, part0(lam2_ref, 2))

    def last_row(i, west0):
        out, p0, gaps1 = retreat_row(lam1_ref, i, west0)
        lam = lam2_ref[i]
        gaps2 = (lam2_ref[i + 1] - lam, next_lat(lam) - lam, next_lev(lam) - lam)
        kappa = kappa_term(gaps2, mid_ref, i) + kappa_term(gaps1, conc_ref, i)
        gc_ref[i - h] = out[PAD:lats - PAD]
        gk_ref[i - h] = kappa[PAD:lats - PAD]
        return p0

    lax.fori_loop(h, rows - h, last_row, part0(lam1_ref, h - 1))


def chain(concentration, wind, kappa, observed):
    lon_rows, lat_rows, levels = concentration.shape
    lat_total = lat_rows * lax.axis_size("lat")
    fields = [concentration, wind[0], wind[1], wind[2], kappa, observed]
    west_rows = (4, 4, 3, 3, 4, 2)
    east_rows = (4, 3, 3, 3, 3, 2)
    got = lon_halo(fields, west_rows, east_rows)
    south, north = lat_halo(fields)
    ext_rows = lon_rows + 2 * HALO
    ext_lats = lat_rows + 2 * PAD
    lat_place = lax.axis_index("lat") * lat_rows - PAD + lax.broadcasted_iota(jnp.int32, (ext_lats, levels), 0)
    north_open = ((lat_place >= 0) & (lat_place < lat_total - 1)).astype(jnp.float32)
    whole = [concentration, wind, kappa, observed, got["west"], got["east"], south, north, north_open]
    vmem = pltpu.MemorySpace.VMEM
    state = pltpu.VMEM((ext_rows, ext_lats, levels), jnp.float32)
    return pl.pallas_call(
        functools.partial(stencil_kernel, west_rows, east_rows),
        out_shape=(
            jax.ShapeDtypeStruct((lon_rows, lat_rows, levels), jnp.float32),
            jax.ShapeDtypeStruct((lon_rows, lat_rows, levels), jnp.float32),
        ),
        in_specs=[pl.BlockSpec(memory_space=vmem) for _ in whole],
        out_specs=(pl.BlockSpec(memory_space=vmem), pl.BlockSpec(memory_space=vmem)),
        scratch_shapes=[
            pltpu.VMEM((len(fields), ext_rows, ext_lats, levels), jnp.float32),
            pltpu.VMEM((3, ext_rows, ext_lats, levels), jnp.float32),
            pltpu.VMEM((3, ext_rows, ext_lats, levels), jnp.float32),
            state,
            state,
            state,
        ],
        compiler_params=pltpu.CompilerParams(vmem_limit_bytes=60 * 1024 * 1024),
    )(*whole)


def solution(mesh):
    return step(mesh)


def step(mesh):
    return jax.shard_map(
        chain,
        mesh=mesh,
        in_specs=(
            P("lon", "lat", None),
            P(None, "lon", "lat", None),
            P("lon", "lat", None),
            P("lon", "lat", None),
        ),
        out_specs=(P("lon", "lat", None), P("lon", "lat", None)),
        check_vma=False,
    )
```

```python
import functools

import jax
import jax.numpy as jnp
from jax import lax
from jax.experimental import pallas as pl
from jax.experimental.pallas import tpu as pltpu
from jax.sharding import PartitionSpec as P

HALO = 4
PAD = 8


def passed_along(value, axis, steps, periodic):
    count = lax.axis_size(axis)
    if periodic:
        pairs = [(source, (source + steps) % count) for source in range(count)]
    else:
        pairs = [(source, source + steps) for source in range(count) if 0 <= source + steps < count]
    return lax.ppermute(value, axis, pairs)


def pack_kernel(west_rows, east_rows, conc, wind, kappa, observed, to_west, to_east, lows, highs):
    fields = [conc, wind.at[0], wind.at[1], wind.at[2], kappa, observed]
    size = conc.shape[0]
    lats = conc.shape[1]
    for out, rows, first in ((to_west, east_rows, True), (to_east, west_rows, False)):
        part = conc[0:rows[0]] if first else conc[size - rows[0]:size]
        high = part.astype(jnp.bfloat16)
        out[0:rows[0]] = high
        out[rows[0]:2 * rows[0]] = (part - high.astype(jnp.float32)).astype(jnp.bfloat16)
        at = 2 * rows[0]
        for f, r in zip(fields[1:], rows[1:]):
            out[at:at + r] = f[0:r] if first else f[size - r:size]
            at += r
    for n, f in enumerate(fields):
        lows[n] = f[:, 0:HALO].astype(jnp.float32)
        highs[n] = f[:, lats - HALO:lats].astype(jnp.float32)


def lat_halo(lows, highs, block):
    from_south = passed_along(highs, "lat", 1, False)
    from_north = passed_along(lows, "lat", -1, False)
    both = jnp.stack([from_south, from_north])
    west = passed_along(both[:, :, block - HALO:], "lon", 1, True)
    east = passed_along(both[:, :, :HALO], "lon", -1, True)
    return [jnp.concatenate([west[n], both[n], east[n]], 1) for n in range(2)]


def stencil_kernel(west_rows, east_rows, conc_in, wind_in, kappa_in, obs_in, west_p, east_p,
                   south_ref, north_halo, north_ref, gc_ref, gk_ref, raw_ref, own_ref, oth_ref, mid_ref, lam2_ref,
                   lam1_ref):
    fields, rows, lats, levels = raw_ref.shape
    block = conc_in.shape[0]
    f32 = jnp.float32
    north_open = north_ref[...]
    lo = PAD
    hi = lats - PAD
    gap = jnp.zeros((PAD - HALO, levels), f32)

    def put(f, r, core):
        raw_ref[f, r, lo:hi] = core
        raw_ref[f, r, lo - HALO:lo] = south_ref[f, r]
        raw_ref[f, r, hi:hi + HALO] = north_halo[f, r]
        raw_ref[f, r, :lo - HALO] = gap
        raw_ref[f, r, hi + HALO:] = gap

    def own_row(i, carry):
        put(0, i + HALO, conc_in[i])
        for d in range(3):
            put(1 + d, i + HALO, wind_in[d, i].astype(f32))
        put(4, i + HALO, kappa_in[i].astype(f32))
        put(5, i + HALO, obs_in[i].astype(f32))
        return carry

    lax.fori_loop(0, block, own_row, 0)
    empty = jnp.zeros((hi - lo, levels), f32)
    for r in range(HALO):
        put(0, r, west_p[r].astype(f32) + west_p[HALO + r].astype(f32))
        put(0, HALO + block + r, east_p[r].astype(f32) + east_p[HALO + r].astype(f32))
    at_w = 2 * HALO
    at_e = 2 * HALO
    for f in range(1, fields):
        w = west_rows[f]
        e = east_rows[f]
        for r in range(HALO):
            put(f, r, west_p[at_w + r - (HALO - w)].astype(f32) if r >= HALO - w else empty)
            put(f, HALO + block + r, east_p[at_e + r].astype(f32) if r < e else empty)
        at_w += w
        at_e += e
    conc_ref = raw_ref.at[0]
    obs_ref = raw_ref.at[5]
    upper_open = (lax.broadcasted_iota(jnp.int32, (lats, levels), 1) < levels - 1).astype(f32)

    def next_lat(f):
        return pltpu.roll(f, lats - 1, 0)

    def back_lat(f):
        return pltpu.roll(f, 1, 0)

    def next_lev(f):
        return pltpu.roll(f, levels - 1, 1)

    def back_lev(f):
        return pltpu.roll(f, 1, 1)

    def coef_row(i, carry):
        diffuse = raw_ref[4, i]
        for d, opened in ((0, None), (1, north_open), (2, upper_open)):
            speed = raw_ref[1 + d, i]
            own = jnp.maximum(speed, 0.0) + diffuse
            oth = jnp.minimum(speed, 0.0) - diffuse
            if opened is not None:
                own = own * opened
                oth = oth * opened
            own_ref[d, i] = own
            oth_ref[d, i] = oth
        return carry

    lax.fori_loop(0, rows, coef_row, 0)

    def flux0(src, i):
        return own_ref[0, i] * src[i] + oth_ref[0, i] * src[i + 1]

    def advance(src, dst, lo, hi, minus=None):
        def row(i, west0):
            c = src[i]
            f0 = own_ref[0, i] * c + oth_ref[0, i] * src[i + 1]
            f1 = own_ref[1, i] * c + oth_ref[1, i] * next_lat(c)
            f2 = own_ref[2, i] * c + oth_ref[2, i] * next_lev(c)
            out = c - (f0 + f1 + f2) + (west0 + back_lat(f1) + back_lev(f2))
            if minus is not None:
                out = out - minus[i]
            dst[i] = out
            return f0

        lax.fori_loop(lo, hi, row, flux0(src, lo - 1))

    def part0(src, i):
        return oth_ref[0, i] * (src[i + 1] - src[i])

    def retreat_row(src, i, west0):
        lam = src[i]
        g0 = src[i + 1] - lam
        g1 = next_lat(lam) - lam
        g2 = next_lev(lam) - lam
        p0 = oth_ref[0, i] * g0
        p1 = oth_ref[1, i] * g1
        p2 = oth_ref[2, i] * g2
        gained = own_ref[0, i] * g0 + own_ref[1, i] * g1 + own_ref[2, i] * g2
        return lam + gained + (west0 + back_lat(p1) + back_lev(p2)), p0, (g0, g1, g2)

    def kappa_term(gaps, state, i):
        c = state[i]
        return (
            gaps[0] * (c - state[i + 1])
            + gaps[1] * (c - next_lat(c)) * north_open
            + gaps[2] * (c - next_lev(c)) * upper_open
        )

    h = (rows - gc_ref.shape[0]) // 2
    advance(conc_ref, mid_ref, 1, rows - 1)
    advance(mid_ref, lam2_ref, 2, rows - 2, minus=obs_ref)

    def lam1_row(i, west0):
        out, p0, _ = retreat_row(lam2_ref, i, west0)
        lam1_ref[i] = out
        return p0

    lax.fori_loop(3, rows - 3, lam1_row, part0(lam2_ref, 2))

    def last_row(i, west0):
        out, p0, gaps1 = retreat_row(lam1_ref, i, west0)
        lam = lam2_ref[i]
        gaps2 = (lam2_ref[i + 1] - lam, next_lat(lam) - lam, next_lev(lam) - lam)
        kappa = kappa_term(gaps2, mid_ref, i) + kappa_term(gaps1, conc_ref, i)
        gc_ref[i - h] = out[PAD:lats - PAD]
        gk_ref[i - h] = kappa[PAD:lats - PAD]
        return p0

    lax.fori_loop(h, rows - h, last_row, part0(lam1_ref, h - 1))


def chain(concentration, wind, kappa, observed):
    lon_rows, lat_rows, levels = concentration.shape
    lat_total = lat_rows * lax.axis_size("lat")
    fields = [concentration, wind[0], wind[1], wind[2], kappa, observed]
    west_rows = (4, 4, 3, 3, 4, 2)
    east_rows = (4, 3, 3, 3, 3, 2)
    vmem = pltpu.MemorySpace.VMEM
    pack_rows = lambda rows: 2 * rows[0] + sum(rows[1:])
    lat_type = jax.ShapeDtypeStruct((len(fields), lon_rows, HALO, levels), jnp.float32)
    to_west, to_east, lows, highs = pl.pallas_call(
        functools.partial(pack_kernel, west_rows, east_rows),
        out_shape=(
            jax.ShapeDtypeStruct((pack_rows(east_rows), lat_rows, levels), jnp.bfloat16),
            jax.ShapeDtypeStruct((pack_rows(west_rows), lat_rows, levels), jnp.bfloat16),
            lat_type,
            lat_type,
        ),
        in_specs=[pl.BlockSpec(memory_space=vmem)] * 4,
        out_specs=tuple(pl.BlockSpec(memory_space=vmem) for _ in range(4)),
    )(concentration, wind, kappa, observed)
    got = {"east": passed_along(to_west, "lon", -1, True), "west": passed_along(to_east, "lon", 1, True)}
    south, north = lat_halo(lows, highs, lon_rows)
    ext_rows = lon_rows + 2 * HALO
    ext_lats = lat_rows + 2 * PAD
    lat_place = lax.axis_index("lat") * lat_rows - PAD + lax.broadcasted_iota(jnp.int32, (ext_lats, levels), 0)
    north_open = ((lat_place >= 0) & (lat_place < lat_total - 1)).astype(jnp.float32)
    whole = [concentration, wind, kappa, observed, got["west"], got["east"], south, north, north_open]
    vmem = pltpu.MemorySpace.VMEM
    state = pltpu.VMEM((ext_rows, ext_lats, levels), jnp.float32)
    return pl.pallas_call(
        functools.partial(stencil_kernel, west_rows, east_rows),
        out_shape=(
            jax.ShapeDtypeStruct((lon_rows, lat_rows, levels), jnp.float32),
            jax.ShapeDtypeStruct((lon_rows, lat_rows, levels), jnp.float32),
        ),
        in_specs=[pl.BlockSpec(memory_space=vmem) for _ in whole],
        out_specs=(pl.BlockSpec(memory_space=vmem), pl.BlockSpec(memory_space=vmem)),
        scratch_shapes=[
            pltpu.VMEM((len(fields), ext_rows, ext_lats, levels), jnp.float32),
            pltpu.VMEM((3, ext_rows, ext_lats, levels), jnp.float32),
            pltpu.VMEM((3, ext_rows, ext_lats, levels), jnp.float32),
            state,
            state,
            state,
        ],
        compiler_params=pltpu.CompilerParams(vmem_limit_bytes=60 * 1024 * 1024),
    )(*whole)


def solution(mesh):
    return step(mesh)


def step(mesh):
    return jax.shard_map(
        chain,
        mesh=mesh,
        in_specs=(
            P("lon", "lat", None),
            P(None, "lon", "lat", None),
            P("lon", "lat", None),
            P("lon", "lat", None),
        ),
        out_specs=(P("lon", "lat", None), P("lon", "lat", None)),
        check_vma=False,
    )
```

```python
import functools

import jax
import jax.numpy as jnp
from jax import lax
from jax.experimental import pallas as pl
from jax.experimental.pallas import tpu as pltpu
from jax.sharding import PartitionSpec as P


HALO = 4
PAD = 8


def passed_along(value, axis, steps, periodic):
    count = lax.axis_size(axis)
    if periodic:
        pairs = [(source, (source + steps) % count) for source in range(count)]
    else:
        pairs = [(source, source + steps) for source in range(count) if 0 <= source + steps < count]
    return lax.ppermute(value, axis, pairs)


def pack_kernel(west_rows, east_rows, conc, wind, kappa, observed, to_west, to_east, lows, highs,
                split, edges, sems):
    size, lats = conc.shape[0], conc.shape[1]
    others = [wind.at[0], wind.at[1], wind.at[2], kappa, observed]
    strip = edges.shape[2] // 2
    copies = []
    for out, rows, first in ((to_west, east_rows, True), (to_east, west_rows, False)):
        at = 2 * rows[0]
        for f, r in zip(others, rows[1:]):
            start = 0 if first else size - r
            copies.append(pltpu.make_async_copy(f.at[pl.ds(start, r)], out.at[pl.ds(at, r)], sems.at[len(copies)]))
            at += r
    for n, f in enumerate(others):
        for k, start in enumerate((0, lats - strip)):
            dst = edges.at[n, :, pl.ds(k * strip, strip)]
            copies.append(pltpu.make_async_copy(f.at[:, pl.ds(start, strip)], dst, sems.at[len(copies)]))
    for c in copies:
        c.start()
    outs = []
    for k, (out, rows, first) in enumerate(((to_west, east_rows, True), (to_east, west_rows, False))):
        part = conc[0:rows[0]] if first else conc[size - rows[0]:size]
        high = part.astype(jnp.bfloat16)
        split[k, 0:rows[0]] = high
        split[k, rows[0]:2 * rows[0]] = (part - high.astype(jnp.float32)).astype(jnp.bfloat16)
        outs.append(pltpu.make_async_copy(split.at[k], out.at[pl.ds(0, 2 * rows[0])], sems.at[len(copies) + k]))
        outs[-1].start()
    lows[0] = conc[:, 0:HALO]
    highs[0] = conc[:, lats - HALO:lats]
    for c in copies:
        c.wait()
    for n in range(len(others)):
        lows[1 + n] = edges[n, :, 0:HALO].astype(jnp.float32)
        highs[1 + n] = edges[n, :, 2 * strip - HALO:2 * strip].astype(jnp.float32)
    for c in outs:
        c.wait()


def lat_halo(lows, highs, block):
    from_south = passed_along(highs, "lat", 1, False)
    from_north = passed_along(lows, "lat", -1, False)
    both = jnp.stack([from_south, from_north])
    west = passed_along(both[:, :, block - HALO:], "lon", 1, True)
    east = passed_along(both[:, :, :HALO], "lon", -1, True)
    return [jnp.concatenate([west[n], both[n], east[n]], 1) for n in range(2)]


def stencil_kernel(west_rows, east_rows, conc_in, wind_in, kappa_in, obs_in, west_p, east_p,
                   south_ref, north_halo, north_ref, gc_ref, gk_ref, raw_ref, own_ref, oth_ref, mid_ref, lam2_ref,
                   lam1_ref):
    fields, rows, lats, levels = raw_ref.shape
    block = conc_in.shape[0]
    f32 = jnp.float32
    north_open = north_ref[...]
    lo = PAD
    hi = lats - PAD
    gap = jnp.zeros((PAD - HALO, levels), f32)

    def put(f, r, core):
        raw_ref[f, r, lo:hi] = core
        raw_ref[f, r, lo - HALO:lo] = south_ref[f, r]
        raw_ref[f, r, hi:hi + HALO] = north_halo[f, r]
        raw_ref[f, r, :lo - HALO] = gap
        raw_ref[f, r, hi + HALO:] = gap

    def own_row(i, carry):
        put(0, i + HALO, conc_in[i])
        for d in range(3):
            put(1 + d, i + HALO, wind_in[d, i].astype(f32))
        put(4, i + HALO, kappa_in[i].astype(f32))
        put(5, i + HALO, obs_in[i].astype(f32))
        return carry

    lax.fori_loop(0, block, own_row, 0)
    empty = jnp.zeros((hi - lo, levels), f32)
    for r in range(HALO):
        put(0, r, west_p[r].astype(f32) + west_p[HALO + r].astype(f32))
        put(0, HALO + block + r, east_p[r].astype(f32) + east_p[HALO + r].astype(f32))
    at_w = 2 * HALO
    at_e = 2 * HALO
    for f in range(1, fields):
        w = west_rows[f]
        e = east_rows[f]
        for r in range(HALO):
            put(f, r, west_p[at_w + r - (HALO - w)].astype(f32) if r >= HALO - w else empty)
            put(f, HALO + block + r, east_p[at_e + r].astype(f32) if r < e else empty)
        at_w += w
        at_e += e
    conc_ref = raw_ref.at[0]
    obs_ref = raw_ref.at[5]
    upper_open = (lax.broadcasted_iota(jnp.int32, (lats, levels), 1) < levels - 1).astype(f32)

    def next_lat(f):
        return pltpu.roll(f, lats - 1, 0)

    def back_lat(f):
        return pltpu.roll(f, 1, 0)

    def next_lev(f):
        return pltpu.roll(f, levels - 1, 1)

    def back_lev(f):
        return pltpu.roll(f, 1, 1)

    def coef_row(i, carry):
        diffuse = raw_ref[4, i]
        for d, opened in ((0, None), (1, north_open), (2, upper_open)):
            speed = raw_ref[1 + d, i]
            own = jnp.maximum(speed, 0.0) + diffuse
            oth = jnp.minimum(speed, 0.0) - diffuse
            if opened is not None:
                own = own * opened
                oth = oth * opened
            own_ref[d, i] = own
            oth_ref[d, i] = oth
        return carry

    lax.fori_loop(0, rows, coef_row, 0)

    def flux0(src, i):
        return own_ref[0, i] * src[i] + oth_ref[0, i] * src[i + 1]

    def advance(src, dst, lo, hi, minus=None):
        def row(i, west0):
            c = src[i]
            f0 = own_ref[0, i] * c + oth_ref[0, i] * src[i + 1]
            f1 = own_ref[1, i] * c + oth_ref[1, i] * next_lat(c)
            f2 = own_ref[2, i] * c + oth_ref[2, i] * next_lev(c)
            out = c - (f0 + f1 + f2) + (west0 + back_lat(f1) + back_lev(f2))
            if minus is not None:
                out = out - minus[i]
            dst[i] = out
            return f0

        lax.fori_loop(lo, hi, row, flux0(src, lo - 1))

    def part0(src, i):
        return oth_ref[0, i] * (src[i + 1] - src[i])

    def retreat_row(src, i, west0):
        lam = src[i]
        g0 = src[i + 1] - lam
        g1 = next_lat(lam) - lam
        g2 = next_lev(lam) - lam
        p0 = oth_ref[0, i] * g0
        p1 = oth_ref[1, i] * g1
        p2 = oth_ref[2, i] * g2
        gained = own_ref[0, i] * g0 + own_ref[1, i] * g1 + own_ref[2, i] * g2
        return lam + gained + (west0 + back_lat(p1) + back_lev(p2)), p0, (g0, g1, g2)

    def kappa_term(gaps, state, i):
        c = state[i]
        return (
            gaps[0] * (c - state[i + 1])
            + gaps[1] * (c - next_lat(c)) * north_open
            + gaps[2] * (c - next_lev(c)) * upper_open
        )

    h = (rows - gc_ref.shape[0]) // 2
    advance(conc_ref, mid_ref, 1, rows - 1)
    advance(mid_ref, lam2_ref, 2, rows - 2, minus=obs_ref)

    def lam1_row(i, west0):
        out, p0, _ = retreat_row(lam2_ref, i, west0)
        lam1_ref[i] = out
        return p0

    lax.fori_loop(3, rows - 3, lam1_row, part0(lam2_ref, 2))

    def last_row(i, west0):
        out, p0, gaps1 = retreat_row(lam1_ref, i, west0)
        lam = lam2_ref[i]
        gaps2 = (lam2_ref[i + 1] - lam, next_lat(lam) - lam, next_lev(lam) - lam)
        kappa = kappa_term(gaps2, mid_ref, i) + kappa_term(gaps1, conc_ref, i)
        gc_ref[i - h] = out[PAD:lats - PAD]
        gk_ref[i - h] = kappa[PAD:lats - PAD]
        return p0

    lax.fori_loop(h, rows - h, last_row, part0(lam1_ref, h - 1))


def chain(concentration, wind, kappa, observed):
    lon_rows, lat_rows, levels = concentration.shape
    lat_total = lat_rows * lax.axis_size("lat")
    fields = [concentration, wind[0], wind[1], wind[2], kappa, observed]
    west_rows = (4, 4, 3, 3, 4, 2)
    east_rows = (4, 3, 3, 3, 3, 2)
    vmem = pltpu.MemorySpace.VMEM
    pack_rows = lambda rows: 2 * rows[0] + sum(rows[1:])
    lat_type = jax.ShapeDtypeStruct((len(fields), lon_rows, HALO, levels), jnp.float32)
    to_west, to_east, lows, highs = pl.pallas_call(
        functools.partial(pack_kernel, west_rows, east_rows),
        out_shape=(
            jax.ShapeDtypeStruct((pack_rows(east_rows), lat_rows, levels), jnp.bfloat16),
            jax.ShapeDtypeStruct((pack_rows(west_rows), lat_rows, levels), jnp.bfloat16),
            lat_type,
            lat_type,
        ),
        in_specs=[pl.BlockSpec(memory_space=vmem)] + [pl.BlockSpec(memory_space=pl.ANY)] * 3,
        out_specs=(pl.BlockSpec(memory_space=pl.ANY), pl.BlockSpec(memory_space=pl.ANY),
                   pl.BlockSpec(memory_space=vmem), pl.BlockSpec(memory_space=vmem)),
        scratch_shapes=[
            pltpu.VMEM((2, 2 * HALO, lat_rows, levels), jnp.bfloat16),
            pltpu.VMEM((len(fields) - 1, lon_rows, 4 * HALO * 2, levels), jnp.bfloat16),
            pltpu.SemaphoreType.DMA((32,)),
        ],
    )(concentration, wind, kappa, observed)
    got = {"east": passed_along(to_west, "lon", -1, True), "west": passed_along(to_east, "lon", 1, True)}
    south, north = lat_halo(lows, highs, lon_rows)
    ext_rows = lon_rows + 2 * HALO
    ext_lats = lat_rows + 2 * PAD
    lat_place = lax.axis_index("lat") * lat_rows - PAD + lax.broadcasted_iota(jnp.int32, (ext_lats, levels), 0)
    north_open = ((lat_place >= 0) & (lat_place < lat_total - 1)).astype(jnp.float32)
    whole = [concentration, wind, kappa, observed, got["west"], got["east"], south, north, north_open]
    vmem = pltpu.MemorySpace.VMEM
    state = pltpu.VMEM((ext_rows, ext_lats, levels), jnp.float32)
    return pl.pallas_call(
        functools.partial(stencil_kernel, west_rows, east_rows),
        out_shape=(
            jax.ShapeDtypeStruct((lon_rows, lat_rows, levels), jnp.float32),
            jax.ShapeDtypeStruct((lon_rows, lat_rows, levels), jnp.float32),
        ),
        in_specs=[pl.BlockSpec(memory_space=vmem) for _ in whole],
        out_specs=(pl.BlockSpec(memory_space=vmem), pl.BlockSpec(memory_space=vmem)),
        scratch_shapes=[
            pltpu.VMEM((len(fields), ext_rows, ext_lats, levels), jnp.float32),
            pltpu.VMEM((3, ext_rows, ext_lats, levels), jnp.float32),
            pltpu.VMEM((3, ext_rows, ext_lats, levels), jnp.float32),
            state,
            state,
            state,
        ],
        compiler_params=pltpu.CompilerParams(vmem_limit_bytes=60 * 1024 * 1024),
    )(*whole)


def solution(mesh):
    return step(mesh)


def step(mesh):
    return jax.shard_map(
        chain,
        mesh=mesh,
        in_specs=(
            P("lon", "lat", None),
            P(None, "lon", "lat", None),
            P("lon", "lat", None),
            P("lon", "lat", None),
        ),
        out_specs=(P("lon", "lat", None), P("lon", "lat", None)),
        check_vma=False,
    )
```

```python
import functools

import jax
import jax.numpy as jnp
from jax import lax
from jax.experimental import pallas as pl
from jax.experimental.pallas import tpu as pltpu
from jax.sharding import PartitionSpec as P


HALO = 4
PAD = 8


def passed_along(value, axis, steps, periodic):
    count = lax.axis_size(axis)
    if periodic:
        pairs = [(source, (source + steps) % count) for source in range(count)]
    else:
        pairs = [(source, source + steps) for source in range(count) if 0 <= source + steps < count]
    return lax.ppermute(value, axis, pairs)


def pack_kernel(west_rows, east_rows, conc, wind, kappa, observed, to_west, to_east, lows, highs):
    fields = [conc, wind.at[0], wind.at[1], wind.at[2], kappa, observed]
    size = conc.shape[0]
    lats = conc.shape[1]
    for out, rows, first in ((to_west, east_rows, True), (to_east, west_rows, False)):
        part = conc[0:rows[0]] if first else conc[size - rows[0]:size]
        high = part.astype(jnp.bfloat16)
        out[0:rows[0]] = high
        out[rows[0]:2 * rows[0]] = (part - high.astype(jnp.float32)).astype(jnp.bfloat16)
        at = 2 * rows[0]
        for f, r in zip(fields[1:], rows[1:]):
            out[at:at + r] = f[0:r] if first else f[size - r:size]
            at += r
    for n, f in enumerate(fields):
        lows[n] = f[:, 0:HALO].astype(jnp.float32)
        highs[n] = f[:, lats - HALO:lats].astype(jnp.float32)


def lat_halo(lows, highs, block):
    from_south = passed_along(highs, "lat", 1, False)
    from_north = passed_along(lows, "lat", -1, False)
    both = jnp.stack([from_south, from_north])
    west = passed_along(both[:, :, block - HALO:], "lon", 1, True)
    east = passed_along(both[:, :, :HALO], "lon", -1, True)
    return west, both, east


def stencil_kernel(west_rows, east_rows, lat_limits, conc_in, wind_in, kappa_in, obs_in, west_p, east_p,
                   corner_w, lat_own, corner_e, place_ref, gc_ref, gk_ref, raw_ref, own_ref, oth_ref, mid_ref,
                   lam2_ref, lam1_ref):
    fields, rows, lats, levels = raw_ref.shape
    block = conc_in.shape[0]
    f32 = jnp.float32
    lat_place = place_ref[0] + lax.broadcasted_iota(jnp.int32, (lats, levels), 0)
    north_open = ((lat_place >= 0) & (lat_place < lat_limits - 1)).astype(f32)
    lo = PAD
    hi = lats - PAD
    gap = jnp.zeros((PAD - HALO, levels), f32)

    def put(f, r, core, halo, at):
        raw_ref[f, r, lo:hi] = core
        raw_ref[f, r, lo - HALO:lo] = halo[0, f, at]
        raw_ref[f, r, hi:hi + HALO] = halo[1, f, at]
        raw_ref[f, r, :lo - HALO] = gap
        raw_ref[f, r, hi + HALO:] = gap

    def own_row(i, carry):
        put(0, i + HALO, conc_in[i], lat_own, i)
        for d in range(3):
            put(1 + d, i + HALO, wind_in[d, i].astype(f32), lat_own, i)
        put(4, i + HALO, kappa_in[i].astype(f32), lat_own, i)
        put(5, i + HALO, obs_in[i].astype(f32), lat_own, i)
        return carry

    lax.fori_loop(0, block, own_row, 0)
    empty = jnp.zeros((hi - lo, levels), f32)
    for r in range(HALO):
        put(0, r, west_p[r].astype(f32) + west_p[HALO + r].astype(f32), corner_w, r)
        put(0, HALO + block + r, east_p[r].astype(f32) + east_p[HALO + r].astype(f32), corner_e, r)
    at_w = 2 * HALO
    at_e = 2 * HALO
    for f in range(1, fields):
        w = west_rows[f]
        e = east_rows[f]
        for r in range(HALO):
            put(f, r, west_p[at_w + r - (HALO - w)].astype(f32) if r >= HALO - w else empty, corner_w, r)
            put(f, HALO + block + r, east_p[at_e + r].astype(f32) if r < e else empty, corner_e, r)
        at_w += w
        at_e += e
    conc_ref = raw_ref.at[0]
    obs_ref = raw_ref.at[5]
    upper_open = (lax.broadcasted_iota(jnp.int32, (lats, levels), 1) < levels - 1).astype(f32)

    def next_lat(f):
        return pltpu.roll(f, lats - 1, 0)

    def back_lat(f):
        return pltpu.roll(f, 1, 0)

    def next_lev(f):
        return pltpu.roll(f, levels - 1, 1)

    def back_lev(f):
        return pltpu.roll(f, 1, 1)

    def coef_row(i, carry):
        diffuse = raw_ref[4, i]
        for d, opened in ((0, None), (1, north_open), (2, upper_open)):
            speed = raw_ref[1 + d, i]
            own = jnp.maximum(speed, 0.0) + diffuse
            oth = jnp.minimum(speed, 0.0) - diffuse
            if opened is not None:
                own = own * opened
                oth = oth * opened
            own_ref[d, i] = own
            oth_ref[d, i] = oth
        return carry

    lax.fori_loop(0, rows, coef_row, 0)

    def flux0(src, i):
        return own_ref[0, i] * src[i] + oth_ref[0, i] * src[i + 1]

    def advance(src, dst, lo, hi, minus=None):
        def row(i, west0):
            c = src[i]
            f0 = own_ref[0, i] * c + oth_ref[0, i] * src[i + 1]
            f1 = own_ref[1, i] * c + oth_ref[1, i] * next_lat(c)
            f2 = own_ref[2, i] * c + oth_ref[2, i] * next_lev(c)
            out = c - (f0 + f1 + f2) + (west0 + back_lat(f1) + back_lev(f2))
            if minus is not None:
                out = out - minus[i]
            dst[i] = out
            return f0

        lax.fori_loop(lo, hi, row, flux0(src, lo - 1))

    def part0(src, i):
        return oth_ref[0, i] * (src[i + 1] - src[i])

    def retreat_row(src, i, west0):
        lam = src[i]
        g0 = src[i + 1] - lam
        g1 = next_lat(lam) - lam
        g2 = next_lev(lam) - lam
        p0 = oth_ref[0, i] * g0
        p1 = oth_ref[1, i] * g1
        p2 = oth_ref[2, i] * g2
        gained = own_ref[0, i] * g0 + own_ref[1, i] * g1 + own_ref[2, i] * g2
        return lam + gained + (west0 + back_lat(p1) + back_lev(p2)), p0, (g0, g1, g2)

    def kappa_term(gaps, state, i):
        c = state[i]
        return (
            gaps[0] * (c - state[i + 1])
            + gaps[1] * (c - next_lat(c)) * north_open
            + gaps[2] * (c - next_lev(c)) * upper_open
        )

    h = (rows - gc_ref.shape[0]) // 2
    advance(conc_ref, mid_ref, 1, rows - 1)
    advance(mid_ref, lam2_ref, 2, rows - 2, minus=obs_ref)

    def lam1_row(i, west0):
        out, p0, _ = retreat_row(lam2_ref, i, west0)
        lam1_ref[i] = out
        return p0

    lax.fori_loop(3, rows - 3, lam1_row, part0(lam2_ref, 2))

    def last_row(i, west0):
        out, p0, gaps1 = retreat_row(lam1_ref, i, west0)
        lam = lam2_ref[i]
        gaps2 = (lam2_ref[i + 1] - lam, next_lat(lam) - lam, next_lev(lam) - lam)
        kappa = kappa_term(gaps2, mid_ref, i) + kappa_term(gaps1, conc_ref, i)
        gc_ref[i - h] = out[PAD:lats - PAD]
        gk_ref[i - h] = kappa[PAD:lats - PAD]
        return p0

    lax.fori_loop(h, rows - h, last_row, part0(lam1_ref, h - 1))


def chain(concentration, wind, kappa, observed):
    lon_rows, lat_rows, levels = concentration.shape
    lat_total = lat_rows * lax.axis_size("lat")
    fields = [concentration, wind[0], wind[1], wind[2], kappa, observed]
    west_rows = (4, 4, 3, 3, 4, 2)
    east_rows = (4, 3, 3, 3, 3, 2)
    vmem = pltpu.MemorySpace.VMEM
    pack_rows = lambda rows: 2 * rows[0] + sum(rows[1:])
    lat_type = jax.ShapeDtypeStruct((len(fields), lon_rows, HALO, levels), jnp.float32)
    to_west, to_east, lows, highs = pl.pallas_call(
        functools.partial(pack_kernel, west_rows, east_rows),
        out_shape=(
            jax.ShapeDtypeStruct((pack_rows(east_rows), lat_rows, levels), jnp.bfloat16),
            jax.ShapeDtypeStruct((pack_rows(west_rows), lat_rows, levels), jnp.bfloat16),
            lat_type,
            lat_type,
        ),
        in_specs=[pl.BlockSpec(memory_space=vmem)] * 4,
        out_specs=tuple(pl.BlockSpec(memory_space=vmem) for _ in range(4)),
    )(concentration, wind, kappa, observed)
    got = {"east": passed_along(to_west, "lon", -1, True), "west": passed_along(to_east, "lon", 1, True)}
    corner_w, lat_own, corner_e = lat_halo(lows, highs, lon_rows)
    ext_rows = lon_rows + 2 * HALO
    ext_lats = lat_rows + 2 * PAD
    place = jnp.reshape(lax.axis_index("lat") * lat_rows - PAD, (1,)).astype(jnp.int32)
    whole = [concentration, wind, kappa, observed, got["west"], got["east"], corner_w, lat_own, corner_e]
    vmem = pltpu.MemorySpace.VMEM
    state = pltpu.VMEM((ext_rows, ext_lats, levels), jnp.float32)
    return pl.pallas_call(
        functools.partial(stencil_kernel, west_rows, east_rows, lat_total),
        out_shape=(
            jax.ShapeDtypeStruct((lon_rows, lat_rows, levels), jnp.float32),
            jax.ShapeDtypeStruct((lon_rows, lat_rows, levels), jnp.float32),
        ),
        in_specs=[pl.BlockSpec(memory_space=vmem) for _ in whole] + [pl.BlockSpec(memory_space=pltpu.SMEM)],
        out_specs=(pl.BlockSpec(memory_space=vmem), pl.BlockSpec(memory_space=vmem)),
        scratch_shapes=[
            pltpu.VMEM((len(fields), ext_rows, ext_lats, levels), jnp.float32),
            pltpu.VMEM((3, ext_rows, ext_lats, levels), jnp.float32),
            pltpu.VMEM((3, ext_rows, ext_lats, levels), jnp.float32),
            state,
            state,
            state,
        ],
        compiler_params=pltpu.CompilerParams(vmem_limit_bytes=60 * 1024 * 1024),
    )(*whole, place)


def solution(mesh):
    return step(mesh)


def step(mesh):
    return jax.shard_map(
        chain,
        mesh=mesh,
        in_specs=(
            P("lon", "lat", None),
            P(None, "lon", "lat", None),
            P("lon", "lat", None),
            P("lon", "lat", None),
        ),
        out_specs=(P("lon", "lat", None), P("lon", "lat", None)),
        check_vma=False,
    )
```

```python
import functools

import jax
import jax.numpy as jnp
from jax import lax
from jax.experimental import pallas as pl
from jax.experimental.pallas import tpu as pltpu
from jax.sharding import PartitionSpec as P


HALO = 4
PAD = 8


def passed_along(value, axis, steps, periodic):
    count = lax.axis_size(axis)
    if periodic:
        pairs = [(source, (source + steps) % count) for source in range(count)]
    else:
        pairs = [(source, source + steps) for source in range(count) if 0 <= source + steps < count]
    return lax.ppermute(value, axis, pairs)


def pack_kernel(west_rows, east_rows, conc, wind, kappa, observed, to_west, to_east, lows, highs):
    fields = [conc, wind.at[0], wind.at[1], wind.at[2], kappa, observed]
    size = conc.shape[0]
    lats = conc.shape[1]
    for out, rows, first in ((to_west, east_rows, True), (to_east, west_rows, False)):
        part = conc[0:rows[0]] if first else conc[size - rows[0]:size]
        high = part.astype(jnp.bfloat16)
        out[0:rows[0]] = high
        low = (part - high.astype(jnp.float32)).astype(jnp.bfloat16)
        out[rows[0]:2 * rows[0] - 1] = low[0:rows[0] - 1] if first else low[1:rows[0]]
        at = 2 * rows[0] - 1
        for f, r in zip(fields[1:], rows[1:]):
            out[at:at + r] = f[0:r] if first else f[size - r:size]
            at += r
    for n, f in enumerate(fields):
        lows[n] = f[:, 0:HALO].astype(jnp.float32)
        highs[n] = f[:, lats - HALO:lats].astype(jnp.float32)


def lat_halo(lows, highs, block):
    from_south = passed_along(highs, "lat", 1, False)
    from_north = passed_along(lows, "lat", -1, False)
    both = jnp.stack([from_south, from_north])
    west = passed_along(both[:, :, block - HALO:], "lon", 1, True)
    east = passed_along(both[:, :, :HALO], "lon", -1, True)
    return west, both, east


def stencil_kernel(west_rows, east_rows, lat_limits, conc_in, wind_in, kappa_in, obs_in, west_p, east_p,
                   corner_w, lat_own, corner_e, place_ref, gc_ref, gk_ref, raw_ref, own_ref, oth_ref, mid_ref,
                   lam2_ref, lam1_ref):
    fields, rows, lats, levels = raw_ref.shape
    block = conc_in.shape[0]
    f32 = jnp.float32
    lat_place = place_ref[0] + lax.broadcasted_iota(jnp.int32, (lats, levels), 0)
    north_open = ((lat_place >= 0) & (lat_place < lat_limits - 1)).astype(f32)
    lo = PAD
    hi = lats - PAD
    gap = jnp.zeros((PAD - HALO, levels), f32)

    def put(f, r, core, halo, at):
        raw_ref[f, r, lo:hi] = core
        raw_ref[f, r, lo - HALO:lo] = halo[0, f, at]
        raw_ref[f, r, hi:hi + HALO] = halo[1, f, at]
        raw_ref[f, r, :lo - HALO] = gap
        raw_ref[f, r, hi + HALO:] = gap

    def own_row(i, carry):
        put(0, i + HALO, conc_in[i], lat_own, i)
        for d in range(3):
            put(1 + d, i + HALO, wind_in[d, i].astype(f32), lat_own, i)
        put(4, i + HALO, kappa_in[i].astype(f32), lat_own, i)
        put(5, i + HALO, obs_in[i].astype(f32), lat_own, i)
        return carry

    lax.fori_loop(0, block, own_row, 0)
    empty = jnp.zeros((hi - lo, levels), f32)
    for r in range(HALO):
        west_c = west_p[r].astype(f32)
        if r >= 1:
            west_c = west_c + west_p[HALO + r - 1].astype(f32)
        east_c = east_p[r].astype(f32)
        if r < HALO - 1:
            east_c = east_c + east_p[HALO + r].astype(f32)
        put(0, r, west_c, corner_w, r)
        put(0, HALO + block + r, east_c, corner_e, r)
    at_w = 2 * HALO - 1
    at_e = 2 * HALO - 1
    for f in range(1, fields):
        w = west_rows[f]
        e = east_rows[f]
        for r in range(HALO):
            put(f, r, west_p[at_w + r - (HALO - w)].astype(f32) if r >= HALO - w else empty, corner_w, r)
            put(f, HALO + block + r, east_p[at_e + r].astype(f32) if r < e else empty, corner_e, r)
        at_w += w
        at_e += e
    conc_ref = raw_ref.at[0]
    obs_ref = raw_ref.at[5]
    upper_open = (lax.broadcasted_iota(jnp.int32, (lats, levels), 1) < levels - 1).astype(f32)

    def next_lat(f):
        return pltpu.roll(f, lats - 1, 0)

    def back_lat(f):
        return pltpu.roll(f, 1, 0)

    def next_lev(f):
        return pltpu.roll(f, levels - 1, 1)

    def back_lev(f):
        return pltpu.roll(f, 1, 1)

    def coef_row(i, carry):
        diffuse = raw_ref[4, i]
        for d, opened in ((0, None), (1, north_open), (2, upper_open)):
            speed = raw_ref[1 + d, i]
            own = jnp.maximum(speed, 0.0) + diffuse
            oth = jnp.minimum(speed, 0.0) - diffuse
            if opened is not None:
                own = own * opened
                oth = oth * opened
            own_ref[d, i] = own
            oth_ref[d, i] = oth
        return carry

    lax.fori_loop(0, rows, coef_row, 0)

    def flux0(src, i):
        return own_ref[0, i] * src[i] + oth_ref[0, i] * src[i + 1]

    def advance(src, dst, lo, hi, minus=None):
        def row(i, west0):
            c = src[i]
            f0 = own_ref[0, i] * c + oth_ref[0, i] * src[i + 1]
            f1 = own_ref[1, i] * c + oth_ref[1, i] * next_lat(c)
            f2 = own_ref[2, i] * c + oth_ref[2, i] * next_lev(c)
            out = c - (f0 + f1 + f2) + (west0 + back_lat(f1) + back_lev(f2))
            if minus is not None:
                out = out - minus[i]
            dst[i] = out
            return f0

        lax.fori_loop(lo, hi, row, flux0(src, lo - 1))

    def part0(src, i):
        return oth_ref[0, i] * (src[i + 1] - src[i])

    def retreat_row(src, i, west0):
        lam = src[i]
        g0 = src[i + 1] - lam
        g1 = next_lat(lam) - lam
        g2 = next_lev(lam) - lam
        p0 = oth_ref[0, i] * g0
        p1 = oth_ref[1, i] * g1
        p2 = oth_ref[2, i] * g2
        gained = own_ref[0, i] * g0 + own_ref[1, i] * g1 + own_ref[2, i] * g2
        return lam + gained + (west0 + back_lat(p1) + back_lev(p2)), p0, (g0, g1, g2)

    def kappa_term(gaps, state, i):
        c = state[i]
        return (
            gaps[0] * (c - state[i + 1])
            + gaps[1] * (c - next_lat(c)) * north_open
            + gaps[2] * (c - next_lev(c)) * upper_open
        )

    h = (rows - gc_ref.shape[0]) // 2
    advance(conc_ref, mid_ref, 1, rows - 1)
    advance(mid_ref, lam2_ref, 2, rows - 2, minus=obs_ref)

    def lam1_row(i, west0):
        out, p0, _ = retreat_row(lam2_ref, i, west0)
        lam1_ref[i] = out
        return p0

    lax.fori_loop(3, rows - 3, lam1_row, part0(lam2_ref, 2))

    def last_row(i, west0):
        out, p0, gaps1 = retreat_row(lam1_ref, i, west0)
        lam = lam2_ref[i]
        gaps2 = (lam2_ref[i + 1] - lam, next_lat(lam) - lam, next_lev(lam) - lam)
        kappa = kappa_term(gaps2, mid_ref, i) + kappa_term(gaps1, conc_ref, i)
        gc_ref[i - h] = out[PAD:lats - PAD]
        gk_ref[i - h] = kappa[PAD:lats - PAD]
        return p0

    lax.fori_loop(h, rows - h, last_row, part0(lam1_ref, h - 1))


def chain(concentration, wind, kappa, observed):
    lon_rows, lat_rows, levels = concentration.shape
    lat_total = lat_rows * lax.axis_size("lat")
    fields = [concentration, wind[0], wind[1], wind[2], kappa, observed]
    west_rows = (4, 4, 3, 3, 4, 2)
    east_rows = (4, 3, 3, 3, 3, 2)
    vmem = pltpu.MemorySpace.VMEM
    pack_rows = lambda rows: 2 * rows[0] - 1 + sum(rows[1:])
    lat_type = jax.ShapeDtypeStruct((len(fields), lon_rows, HALO, levels), jnp.float32)
    to_west, to_east, lows, highs = pl.pallas_call(
        functools.partial(pack_kernel, west_rows, east_rows),
        out_shape=(
            jax.ShapeDtypeStruct((pack_rows(east_rows), lat_rows, levels), jnp.bfloat16),
            jax.ShapeDtypeStruct((pack_rows(west_rows), lat_rows, levels), jnp.bfloat16),
            lat_type,
            lat_type,
        ),
        in_specs=[pl.BlockSpec(memory_space=vmem)] * 4,
        out_specs=tuple(pl.BlockSpec(memory_space=vmem) for _ in range(4)),
    )(concentration, wind, kappa, observed)
    got = {"east": passed_along(to_west, "lon", -1, True), "west": passed_along(to_east, "lon", 1, True)}
    corner_w, lat_own, corner_e = lat_halo(lows, highs, lon_rows)
    ext_rows = lon_rows + 2 * HALO
    ext_lats = lat_rows + 2 * PAD
    place = jnp.reshape(lax.axis_index("lat") * lat_rows - PAD, (1,)).astype(jnp.int32)
    whole = [concentration, wind, kappa, observed, got["west"], got["east"], corner_w, lat_own, corner_e]
    vmem = pltpu.MemorySpace.VMEM
    state = pltpu.VMEM((ext_rows, ext_lats, levels), jnp.float32)
    return pl.pallas_call(
        functools.partial(stencil_kernel, west_rows, east_rows, lat_total),
        out_shape=(
            jax.ShapeDtypeStruct((lon_rows, lat_rows, levels), jnp.float32),
            jax.ShapeDtypeStruct((lon_rows, lat_rows, levels), jnp.float32),
        ),
        in_specs=[pl.BlockSpec(memory_space=vmem) for _ in whole] + [pl.BlockSpec(memory_space=pltpu.SMEM)],
        out_specs=(pl.BlockSpec(memory_space=vmem), pl.BlockSpec(memory_space=vmem)),
        scratch_shapes=[
            pltpu.VMEM((len(fields), ext_rows, ext_lats, levels), jnp.float32),
            pltpu.VMEM((3, ext_rows, ext_lats, levels), jnp.float32),
            pltpu.VMEM((3, ext_rows, ext_lats, levels), jnp.float32),
            state,
            state,
            state,
        ],
        compiler_params=pltpu.CompilerParams(vmem_limit_bytes=60 * 1024 * 1024),
    )(*whole, place)


def solution(mesh):
    return step(mesh)


def step(mesh):
    return jax.shard_map(
        chain,
        mesh=mesh,
        in_specs=(
            P("lon", "lat", None),
            P(None, "lon", "lat", None),
            P("lon", "lat", None),
            P("lon", "lat", None),
        ),
        out_specs=(P("lon", "lat", None), P("lon", "lat", None)),
        check_vma=False,
    )
```

```python
import functools

import jax
import jax.numpy as jnp
from jax import lax
from jax.experimental import pallas as pl
from jax.experimental.pallas import tpu as pltpu
from jax.sharding import PartitionSpec as P


HALO = 4
PAD = 8


def passed_along(value, axis, steps, periodic):
    count = lax.axis_size(axis)
    if periodic:
        pairs = [(source, (source + steps) % count) for source in range(count)]
    else:
        pairs = [(source, source + steps) for source in range(count) if 0 <= source + steps < count]
    return lax.ppermute(value, axis, pairs)


def pack_kernel(west_rows, east_rows, conc, wind, kappa, observed, to_west, to_east, lows, highs):
    fields = [conc, wind.at[0], wind.at[1], wind.at[2], kappa, observed]
    size = conc.shape[0]
    lats = conc.shape[1]
    for out, rows, first in ((to_west, east_rows, True), (to_east, west_rows, False)):
        part = conc[0:rows[0]] if first else conc[size - rows[0]:size]
        high = part.astype(jnp.bfloat16)
        out[0:rows[0]] = high
        low = (part - high.astype(jnp.float32)).astype(jnp.bfloat16)
        out[rows[0]:2 * rows[0] - 1] = low[0:rows[0] - 1] if first else low[1:rows[0]]
        at = 2 * rows[0] - 1
        for f, r in zip(fields[1:], rows[1:]):
            out[at:at + r] = f[0:r] if first else f[size - r:size]
            at += r
    for n, f in enumerate(fields):
        lows[n] = f[:, 0:HALO].astype(jnp.float32)
        highs[n] = f[:, lats - HALO:lats].astype(jnp.float32)


def lat_halo(lows, highs, block):
    from_south = passed_along(highs, "lat", 1, False)
    from_north = passed_along(lows, "lat", -1, False)
    both = jnp.stack([from_south, from_north])
    west = passed_along(both[:, :, block - HALO:], "lon", 1, True)
    east = passed_along(both[:, :, :HALO], "lon", -1, True)
    return west, both, east


def stencil_kernel(west_rows, east_rows, lat_limits, conc_in, wind_in, kappa_in, obs_in, west_p, east_p,
                   corner_w, lat_own, corner_e, place_ref, gc_ref, gk_ref, raw_ref, own_ref, oth_ref, mid_ref,
                   lam2_ref, lam1_ref):
    fields, rows, lats, levels = raw_ref.shape
    block = conc_in.shape[0]
    f32 = jnp.float32
    lat_place = place_ref[0] + lax.broadcasted_iota(jnp.int32, (lats, levels), 0)
    north_open = ((lat_place >= 0) & (lat_place < lat_limits - 1)).astype(f32)
    lo = PAD
    hi = lats - PAD
    gap = jnp.zeros((PAD - HALO, levels), f32)

    def put(f, r, core, halo, at):
        raw_ref[f, r, lo:hi] = core
        raw_ref[f, r, lo - HALO:lo] = halo[0, f, at]
        raw_ref[f, r, hi:hi + HALO] = halo[1, f, at]
        raw_ref[f, r, :lo - HALO] = gap
        raw_ref[f, r, hi + HALO:] = gap

    def own_row(i, carry):
        put(0, i + HALO, conc_in[i], lat_own, i)
        for d in range(3):
            put(1 + d, i + HALO, wind_in[d, i].astype(f32), lat_own, i)
        put(4, i + HALO, kappa_in[i].astype(f32), lat_own, i)
        put(5, i + HALO, obs_in[i].astype(f32), lat_own, i)
        return carry

    lax.fori_loop(0, block, own_row, 0)
    empty = jnp.zeros((hi - lo, levels), f32)
    for r in range(HALO):
        west_c = west_p[r].astype(f32)
        if r >= 1:
            west_c = west_c + west_p[HALO + r - 1].astype(f32)
        east_c = east_p[r].astype(f32)
        if r < HALO - 1:
            east_c = east_c + east_p[HALO + r].astype(f32)
        put(0, r, west_c, corner_w, r)
        put(0, HALO + block + r, east_c, corner_e, r)
    at_w = 2 * HALO - 1
    at_e = 2 * HALO - 1
    for f in range(1, fields):
        w = west_rows[f]
        e = east_rows[f]
        for r in range(HALO):
            put(f, r, west_p[at_w + r - (HALO - w)].astype(f32) if r >= HALO - w else empty, corner_w, r)
            put(f, HALO + block + r, east_p[at_e + r].astype(f32) if r < e else empty, corner_e, r)
        at_w += w
        at_e += e
    conc_ref = raw_ref.at[0]
    obs_ref = raw_ref.at[5]
    upper_open = (lax.broadcasted_iota(jnp.int32, (lats, levels), 1) < levels - 1).astype(f32)

    def next_lat(f):
        return pltpu.roll(f, lats - 1, 0)

    def back_lat(f):
        return pltpu.roll(f, 1, 0)

    def next_lev(f):
        return pltpu.roll(f, levels - 1, 1)

    def back_lev(f):
        return pltpu.roll(f, 1, 1)

    def coef_row(i, carry):
        diffuse = raw_ref[4, i]
        for d, opened in ((0, None), (1, north_open), (2, upper_open)):
            speed = raw_ref[1 + d, i]
            own = jnp.maximum(speed, 0.0) + diffuse
            oth = jnp.minimum(speed, 0.0) - diffuse
            if opened is not None:
                own = own * opened
                oth = oth * opened
            own_ref[d, i] = own
            oth_ref[d, i] = oth
        return carry

    lax.fori_loop(0, rows, coef_row, 0, unroll=2)

    def flux0(src, i):
        return own_ref[0, i] * src[i] + oth_ref[0, i] * src[i + 1]

    def advance(src, dst, lo, hi, minus=None):
        def row(i, west0):
            c = src[i]
            f0 = own_ref[0, i] * c + oth_ref[0, i] * src[i + 1]
            f1 = own_ref[1, i] * c + oth_ref[1, i] * next_lat(c)
            f2 = own_ref[2, i] * c + oth_ref[2, i] * next_lev(c)
            out = c - (f0 + f1 + f2) + (west0 + back_lat(f1) + back_lev(f2))
            if minus is not None:
                out = out - minus[i]
            dst[i] = out
            return f0

        lax.fori_loop(lo, hi, row, flux0(src, lo - 1), unroll=2)

    def part0(src, i):
        return oth_ref[0, i] * (src[i + 1] - src[i])

    def retreat_row(src, i, west0):
        lam = src[i]
        g0 = src[i + 1] - lam
        g1 = next_lat(lam) - lam
        g2 = next_lev(lam) - lam
        p0 = oth_ref[0, i] * g0
        p1 = oth_ref[1, i] * g1
        p2 = oth_ref[2, i] * g2
        gained = own_ref[0, i] * g0 + own_ref[1, i] * g1 + own_ref[2, i] * g2
        return lam + gained + (west0 + back_lat(p1) + back_lev(p2)), p0, (g0, g1, g2)

    def kappa_term(gaps, state, i):
        c = state[i]
        return (
            gaps[0] * (c - state[i + 1])
            + gaps[1] * (c - next_lat(c)) * north_open
            + gaps[2] * (c - next_lev(c)) * upper_open
        )

    h = (rows - gc_ref.shape[0]) // 2
    advance(conc_ref, mid_ref, 1, rows - 1)
    advance(mid_ref, lam2_ref, 2, rows - 2, minus=obs_ref)

    def lam1_row(i, west0):
        out, p0, _ = retreat_row(lam2_ref, i, west0)
        lam1_ref[i] = out
        return p0

    lax.fori_loop(3, rows - 3, lam1_row, part0(lam2_ref, 2), unroll=2)

    def last_row(i, west0):
        out, p0, gaps1 = retreat_row(lam1_ref, i, west0)
        lam = lam2_ref[i]
        gaps2 = (lam2_ref[i + 1] - lam, next_lat(lam) - lam, next_lev(lam) - lam)
        kappa = kappa_term(gaps2, mid_ref, i) + kappa_term(gaps1, conc_ref, i)
        gc_ref[i - h] = out[PAD:lats - PAD]
        gk_ref[i - h] = kappa[PAD:lats - PAD]
        return p0

    lax.fori_loop(h, rows - h, last_row, part0(lam1_ref, h - 1), unroll=2)


def chain(concentration, wind, kappa, observed):
    lon_rows, lat_rows, levels = concentration.shape
    lat_total = lat_rows * lax.axis_size("lat")
    fields = [concentration, wind[0], wind[1], wind[2], kappa, observed]
    west_rows = (4, 4, 3, 3, 4, 2)
    east_rows = (4, 3, 3, 3, 3, 2)
    vmem = pltpu.MemorySpace.VMEM
    pack_rows = lambda rows: 2 * rows[0] - 1 + sum(rows[1:])
    lat_type = jax.ShapeDtypeStruct((len(fields), lon_rows, HALO, levels), jnp.float32)
    to_west, to_east, lows, highs = pl.pallas_call(
        functools.partial(pack_kernel, west_rows, east_rows),
        out_shape=(
            jax.ShapeDtypeStruct((pack_rows(east_rows), lat_rows, levels), jnp.bfloat16),
            jax.ShapeDtypeStruct((pack_rows(west_rows), lat_rows, levels), jnp.bfloat16),
            lat_type,
            lat_type,
        ),
        in_specs=[pl.BlockSpec(memory_space=vmem)] * 4,
        out_specs=tuple(pl.BlockSpec(memory_space=vmem) for _ in range(4)),
    )(concentration, wind, kappa, observed)
    got = {"east": passed_along(to_west, "lon", -1, True), "west": passed_along(to_east, "lon", 1, True)}
    corner_w, lat_own, corner_e = lat_halo(lows, highs, lon_rows)
    ext_rows = lon_rows + 2 * HALO
    ext_lats = lat_rows + 2 * PAD
    place = jnp.reshape(lax.axis_index("lat") * lat_rows - PAD, (1,)).astype(jnp.int32)
    whole = [concentration, wind, kappa, observed, got["west"], got["east"], corner_w, lat_own, corner_e]
    vmem = pltpu.MemorySpace.VMEM
    state = pltpu.VMEM((ext_rows, ext_lats, levels), jnp.float32)
    return pl.pallas_call(
        functools.partial(stencil_kernel, west_rows, east_rows, lat_total),
        out_shape=(
            jax.ShapeDtypeStruct((lon_rows, lat_rows, levels), jnp.float32),
            jax.ShapeDtypeStruct((lon_rows, lat_rows, levels), jnp.float32),
        ),
        in_specs=[pl.BlockSpec(memory_space=vmem) for _ in whole] + [pl.BlockSpec(memory_space=pltpu.SMEM)],
        out_specs=(pl.BlockSpec(memory_space=vmem), pl.BlockSpec(memory_space=vmem)),
        scratch_shapes=[
            pltpu.VMEM((len(fields), ext_rows, ext_lats, levels), jnp.float32),
            pltpu.VMEM((3, ext_rows, ext_lats, levels), jnp.float32),
            pltpu.VMEM((3, ext_rows, ext_lats, levels), jnp.float32),
            state,
            state,
            state,
        ],
        compiler_params=pltpu.CompilerParams(vmem_limit_bytes=60 * 1024 * 1024),
    )(*whole, place)


def solution(mesh):
    return step(mesh)


def step(mesh):
    return jax.shard_map(
        chain,
        mesh=mesh,
        in_specs=(
            P("lon", "lat", None),
            P(None, "lon", "lat", None),
            P("lon", "lat", None),
            P("lon", "lat", None),
        ),
        out_specs=(P("lon", "lat", None), P("lon", "lat", None)),
        check_vma=False,
    )
```

```python
import functools

import jax
import jax.numpy as jnp
from jax import lax
from jax.experimental import pallas as pl
from jax.experimental.pallas import tpu as pltpu
from jax.sharding import PartitionSpec as P


HALO = 4
PAD = 8


def passed_along(value, axis, steps, periodic):
    count = lax.axis_size(axis)
    if periodic:
        pairs = [(source, (source + steps) % count) for source in range(count)]
    else:
        pairs = [(source, source + steps) for source in range(count) if 0 <= source + steps < count]
    return lax.ppermute(value, axis, pairs)


def pack_kernel(west_rows, east_rows, conc, wind, kappa, observed, to_west, to_east, lows, highs):
    fields = [conc, wind.at[0], wind.at[1], wind.at[2], kappa, observed]
    size = conc.shape[0]
    lats = conc.shape[1]
    for out, rows, first in ((to_west, east_rows, True), (to_east, west_rows, False)):
        part = conc[0:rows[0]] if first else conc[size - rows[0]:size]
        high = part.astype(jnp.bfloat16)
        out[0:rows[0]] = high
        low = (part - high.astype(jnp.float32)).astype(jnp.bfloat16)
        out[rows[0]:2 * rows[0] - 1] = low[0:rows[0] - 1] if first else low[1:rows[0]]
        at = 2 * rows[0] - 1
        for f, r in zip(fields[1:], rows[1:]):
            out[at:at + r] = f[0:r] if first else f[size - r:size]
            at += r
    for n, f in enumerate(fields):
        lows[n] = f[:, 0:HALO].astype(jnp.float32)
        highs[n] = f[:, lats - HALO:lats].astype(jnp.float32)


def lat_halo(lows, highs, block):
    from_south = passed_along(highs, "lat", 1, False)
    from_north = passed_along(lows, "lat", -1, False)
    both = jnp.stack([from_south, from_north])
    west = passed_along(both[:, :, block - HALO:], "lon", 1, True)
    east = passed_along(both[:, :, :HALO], "lon", -1, True)
    return west, both, east


def stencil_kernel(west_rows, east_rows, lat_limits, conc_in, wind_in, kappa_in, obs_in, west_p, east_p,
                   corner_w, lat_own, corner_e, place_ref, gc_ref, gk_ref, raw_ref, own_ref, oth_ref, mid_ref,
                   lam2_ref, lam1_ref):
    fields, rows, lats, levels = raw_ref.shape
    block = conc_in.shape[0]
    f32 = jnp.float32
    lat_place = place_ref[0] + lax.broadcasted_iota(jnp.int32, (lats, levels), 0)
    north_open = ((lat_place >= 0) & (lat_place < lat_limits - 1)).astype(f32)
    lo = PAD
    hi = lats - PAD
    gap = jnp.zeros((PAD - HALO, levels), f32)

    def put(f, r, core, halo, at):
        raw_ref[f, r, lo:hi] = core
        raw_ref[f, r, lo - HALO:lo] = halo[0, f, at]
        raw_ref[f, r, hi:hi + HALO] = halo[1, f, at]
        raw_ref[f, r, :lo - HALO] = gap
        raw_ref[f, r, hi + HALO:] = gap

    def own_row(i, carry):
        put(0, i + HALO, conc_in[i], lat_own, i)
        for d in range(3):
            put(1 + d, i + HALO, wind_in[d, i].astype(f32), lat_own, i)
        put(4, i + HALO, kappa_in[i].astype(f32), lat_own, i)
        put(5, i + HALO, obs_in[i].astype(f32), lat_own, i)
        return carry

    lax.fori_loop(0, block, own_row, 0)
    empty = jnp.zeros((hi - lo, levels), f32)
    for r in range(HALO):
        west_c = west_p[r].astype(f32)
        if r >= 1:
            west_c = west_c + west_p[HALO + r - 1].astype(f32)
        east_c = east_p[r].astype(f32)
        if r < HALO - 1:
            east_c = east_c + east_p[HALO + r].astype(f32)
        put(0, r, west_c, corner_w, r)
        put(0, HALO + block + r, east_c, corner_e, r)
    at_w = 2 * HALO - 1
    at_e = 2 * HALO - 1
    for f in range(1, fields):
        w = west_rows[f]
        e = east_rows[f]
        for r in range(HALO):
            put(f, r, west_p[at_w + r - (HALO - w)].astype(f32) if r >= HALO - w else empty, corner_w, r)
            put(f, HALO + block + r, east_p[at_e + r].astype(f32) if r < e else empty, corner_e, r)
        at_w += w
        at_e += e
    conc_ref = raw_ref.at[0]
    obs_ref = raw_ref.at[5]
    upper_open = (lax.broadcasted_iota(jnp.int32, (lats, levels), 1) < levels - 1).astype(f32)

    def next_lat(f):
        return pltpu.roll(f, lats - 1, 0)

    def back_lat(f):
        return pltpu.roll(f, 1, 0)

    def next_lev(f):
        return pltpu.roll(f, levels - 1, 1)

    def back_lev(f):
        return pltpu.roll(f, 1, 1)

    def coef_row(i, carry):
        diffuse = raw_ref[4, i]
        for d, opened in ((0, None), (1, north_open), (2, upper_open)):
            speed = raw_ref[1 + d, i]
            own = jnp.maximum(speed, 0.0) + diffuse
            oth = jnp.minimum(speed, 0.0) - diffuse
            if opened is not None:
                own = own * opened
                oth = oth * opened
            own_ref[d, i] = own
            oth_ref[d, i] = oth
        return carry

    lax.fori_loop(0, rows, coef_row, 0, unroll=4)

    def flux0(src, i):
        return own_ref[0, i] * src[i] + oth_ref[0, i] * src[i + 1]

    def advance(src, dst, lo, hi, minus=None):
        def row(i, west0):
            c = src[i]
            f0 = own_ref[0, i] * c + oth_ref[0, i] * src[i + 1]
            f1 = own_ref[1, i] * c + oth_ref[1, i] * next_lat(c)
            f2 = own_ref[2, i] * c + oth_ref[2, i] * next_lev(c)
            out = c - (f0 + f1 + f2) + (west0 + back_lat(f1) + back_lev(f2))
            if minus is not None:
                out = out - minus[i]
            dst[i] = out
            return f0

        lax.fori_loop(lo, hi, row, flux0(src, lo - 1), unroll=4)

    def part0(src, i):
        return oth_ref[0, i] * (src[i + 1] - src[i])

    def retreat_row(src, i, west0):
        lam = src[i]
        g0 = src[i + 1] - lam
        g1 = next_lat(lam) - lam
        g2 = next_lev(lam) - lam
        p0 = oth_ref[0, i] * g0
        p1 = oth_ref[1, i] * g1
        p2 = oth_ref[2, i] * g2
        gained = own_ref[0, i] * g0 + own_ref[1, i] * g1 + own_ref[2, i] * g2
        return lam + gained + (west0 + back_lat(p1) + back_lev(p2)), p0, (g0, g1, g2)

    def kappa_term(gaps, state, i):
        c = state[i]
        return (
            gaps[0] * (c - state[i + 1])
            + gaps[1] * (c - next_lat(c)) * north_open
            + gaps[2] * (c - next_lev(c)) * upper_open
        )

    h = (rows - gc_ref.shape[0]) // 2
    advance(conc_ref, mid_ref, 1, rows - 1)
    advance(mid_ref, lam2_ref, 2, rows - 2, minus=obs_ref)

    def lam1_row(i, west0):
        out, p0, _ = retreat_row(lam2_ref, i, west0)
        lam1_ref[i] = out
        return p0

    lax.fori_loop(3, rows - 3, lam1_row, part0(lam2_ref, 2), unroll=4)

    def last_row(i, west0):
        out, p0, gaps1 = retreat_row(lam1_ref, i, west0)
        lam = lam2_ref[i]
        gaps2 = (lam2_ref[i + 1] - lam, next_lat(lam) - lam, next_lev(lam) - lam)
        kappa = kappa_term(gaps2, mid_ref, i) + kappa_term(gaps1, conc_ref, i)
        gc_ref[i - h] = out[PAD:lats - PAD]
        gk_ref[i - h] = kappa[PAD:lats - PAD]
        return p0

    lax.fori_loop(h, rows - h, last_row, part0(lam1_ref, h - 1), unroll=4)


def chain(concentration, wind, kappa, observed):
    lon_rows, lat_rows, levels = concentration.shape
    lat_total = lat_rows * lax.axis_size("lat")
    fields = [concentration, wind[0], wind[1], wind[2], kappa, observed]
    west_rows = (4, 4, 3, 3, 4, 2)
    east_rows = (4, 3, 3, 3, 3, 2)
    vmem = pltpu.MemorySpace.VMEM
    pack_rows = lambda rows: 2 * rows[0] - 1 + sum(rows[1:])
    lat_type = jax.ShapeDtypeStruct((len(fields), lon_rows, HALO, levels), jnp.float32)
    to_west, to_east, lows, highs = pl.pallas_call(
        functools.partial(pack_kernel, west_rows, east_rows),
        out_shape=(
            jax.ShapeDtypeStruct((pack_rows(east_rows), lat_rows, levels), jnp.bfloat16),
            jax.ShapeDtypeStruct((pack_rows(west_rows), lat_rows, levels), jnp.bfloat16),
            lat_type,
            lat_type,
        ),
        in_specs=[pl.BlockSpec(memory_space=vmem)] * 4,
        out_specs=tuple(pl.BlockSpec(memory_space=vmem) for _ in range(4)),
    )(concentration, wind, kappa, observed)
    got = {"east": passed_along(to_west, "lon", -1, True), "west": passed_along(to_east, "lon", 1, True)}
    corner_w, lat_own, corner_e = lat_halo(lows, highs, lon_rows)
    ext_rows = lon_rows + 2 * HALO
    ext_lats = lat_rows + 2 * PAD
    place = jnp.reshape(lax.axis_index("lat") * lat_rows - PAD, (1,)).astype(jnp.int32)
    whole = [concentration, wind, kappa, observed, got["west"], got["east"], corner_w, lat_own, corner_e]
    vmem = pltpu.MemorySpace.VMEM
    state = pltpu.VMEM((ext_rows, ext_lats, levels), jnp.float32)
    return pl.pallas_call(
        functools.partial(stencil_kernel, west_rows, east_rows, lat_total),
        out_shape=(
            jax.ShapeDtypeStruct((lon_rows, lat_rows, levels), jnp.float32),
            jax.ShapeDtypeStruct((lon_rows, lat_rows, levels), jnp.float32),
        ),
        in_specs=[pl.BlockSpec(memory_space=vmem) for _ in whole] + [pl.BlockSpec(memory_space=pltpu.SMEM)],
        out_specs=(pl.BlockSpec(memory_space=vmem), pl.BlockSpec(memory_space=vmem)),
        scratch_shapes=[
            pltpu.VMEM((len(fields), ext_rows, ext_lats, levels), jnp.float32),
            pltpu.VMEM((3, ext_rows, ext_lats, levels), jnp.float32),
            pltpu.VMEM((3, ext_rows, ext_lats, levels), jnp.float32),
            state,
            state,
            state,
        ],
        compiler_params=pltpu.CompilerParams(vmem_limit_bytes=60 * 1024 * 1024),
    )(*whole, place)


def solution(mesh):
    return step(mesh)


def step(mesh):
    return jax.shard_map(
        chain,
        mesh=mesh,
        in_specs=(
            P("lon", "lat", None),
            P(None, "lon", "lat", None),
            P("lon", "lat", None),
            P("lon", "lat", None),
        ),
        out_specs=(P("lon", "lat", None), P("lon", "lat", None)),
        check_vma=False,
    )
```
